512 devices in a mesh: dp: 64 (over x, y, core), mp: 8 (over z).
Axes of the slice: x: 4, y: 8, z: 8, core: 2. Of those that a mesh axis runs over, the one named last changes fastest.
Arguments:
- corpus: bfloat16 [8192, 16, 320], P('dp'), may hold values from -6 to 6
- picks: int32 [64, 64], P('dp'), may hold values from 0 to 127
- lengths: int32 [8192], P('dp'), may hold values from 1 to 16, 98304 in all
- langs: int32 [8192], P('dp'), may hold values from 0 to 127
- w_in: bfloat16 [320, 1536], P(None, 'mp'), may hold values from -0.3125 to 0.3125
- lang_table: bfloat16 [128, 1536], P(None, 'mp'), may hold values from -3 to 3
- ln_gain: float32 [1536], P('mp'), may hold values from 0.1 to 1.9
- w_pw1: bfloat16 [1536, 2, 1536], P('dp', None, 'mp'), may hold values from -0.15625 to 0.15625
- kernel: float32 [31, 1536], P(None, 'mp'), may hold values from -1.5 to 1.5
- bn_gain: float32 [1536], P('mp'), may hold values from 0.1 to 1.9
- bn_bias: float32 [1536], P('mp'), may hold values from -3 to 3
- w_pw2: bfloat16 [1536, 1536], P('dp', 'mp'), may hold values from -0.15625 to 0.15625
- cotangent: bfloat16 [65536, 1536], P('dp', 'mp'), may hold values from -6 to 6
Outputs:
- encoded: bfloat16 [65536, 1536], P('dp', 'mp')
- grad_pw1: float32 [1536, 2, 1536], P('dp', None, 'mp')
- grad_pw2: float32 [1536, 1536], P('dp', 'mp')
- grad_kernel: float32 [31, 1536], P(None, 'mp')
- grad_bn_gain: float32 [1536], P('mp')
- grad_bn_bias: float32 [1536], P('mp')
The draws below stay inside these ranges and needn't reach their ends.
Inputs may be any that keep to these rules, and one draw needn't show every extreme that they name: `picks`: each trainer takes one block of every shard; a shard may give the same block to several trainers.
All inputs are finite; a program needn't handle non-finite values. No bound on the sum of `lengths` on one device may be relied on, other than what follows from the above.
Results may differ from the reference program's by a relative error of at most 0.0057.
Values may be sent and summed in bfloat16 or wider, within the bound.
No kernel may reach another device: no remote copies, remote signals or barrier semaphores. Data moves between devices by JAX's collectives and lax.ppermute only.
A program may use at most 64 MiB of HBM per device.

```python
import math
import jax
import jax.numpy as jnp
import numpy as np
from jax import lax

D = 1536
FEAT = 320
LANGS = 128
KER = 31
BLK = 16
CB = 128
TOTAL_ROWS = 65536
CORPUS = 8192
N_DP = 64


def with_ends(entries, key, smallest, top_value):
    longest = entries.shape.index(max(entries.shape))
    spots = []
    for shift in (0, 1):
        where = [jax.random.randint(jax.random.fold_in(key, axis), (), 0, length) for axis, length in enumerate(entries.shape)]
        where[longest] = (where[longest] + shift) % entries.shape[longest]
        spots.append(tuple(where))
    return entries.at[spots[0]].set(smallest).at[spots[1]].set(top_value)


def block_scale(own_key, dims, split, smallest, largest):
    level, own = 1.0, jax.random.fold_in(own_key, 6)
    for axis_at, shards_of in split:
        steps = jnp.exp(jax.random.uniform(jax.random.fold_in(own, axis_at), (shards_of,), jnp.float32, smallest / len(split), largest / len(split)))
        level = level * jnp.repeat(steps, dims[axis_at] // shards_of).reshape([-1 if axis == axis_at else 1 for axis in range(len(dims))])
    return level


def split_up(number_of, total, reach, lean):
    portions = [(1 << 20) // math.isqrt(standing ** lean) + 1 for standing in range(2, number_of + 1)]
    rest, given = total - reach - (number_of - 1), [1] * (number_of - 1)
    while rest > 0:
        candidates = [i for i in range(number_of - 1) if given[i] < reach]
        whole, remaining = sum([portions[i] for i in candidates]), rest
        for i in candidates:
            extra = min(reach - given[i], max(1, remaining * portions[i] // whole), rest)
            given[i] = given[i] + extra
            rest = rest - extra
    return np.array([reach] + given)


def uneven(stream_key, number_of, total, reach, lean):
    if number_of == 2:
        one = jax.random.randint(stream_key, (), max(1, total - reach), min(reach, total - 1) + 1)
        return jnp.stack([one, total - one])
    sizes = jnp.asarray(split_up(number_of, total, reach, lean), jnp.int32)
    couples = (number_of - 1) // 2
    donor, sink = sizes[1:1 + 2 * couples:2], sizes[2:2 + 2 * couples:2]
    room = jnp.minimum(donor - 1, reach - sink)
    passed = jax.random.randint(jax.random.fold_in(stream_key, 1), (couples,), 0, 1 << 20) % (room + 1)
    sizes = sizes.at[1:1 + 2 * couples:2].set(donor - passed).at[2:2 + 2 * couples:2].set(sink + passed)
    return sizes[jax.random.permutation(jax.random.fold_in(stream_key, 2), number_of)]


def scatter_about(rng, dims, scale, most, pieces=(), kind=jnp.bfloat16):
    drawn = scale * jax.random.normal(rng, dims, jnp.float32)
    if pieces:
        drawn = drawn * block_scale(rng, dims, pieces, -0.22, 0.18)
    return jnp.clip(drawn, -most, most).astype(kind)


def setup_inputs(seed: int = 0) -> dict:
    arg_keys = jax.random.split(jax.random.key(seed), 14)
    corpus = scatter_about(arg_keys[0], (CORPUS, BLK, FEAT), 1.0, 6.0, ((0, 64),))
    picks = with_ends(jax.random.randint(arg_keys[1], (N_DP, N_DP), 0, CB), jax.random.fold_in(arg_keys[1], 1), 0, CB - 1).astype(jnp.int32)
    lengths = uneven(arg_keys[2], CORPUS, CORPUS * BLK * 3 // 4, BLK, 1).astype(jnp.int32)
    langs = with_ends(jax.random.randint(arg_keys[3], (CORPUS,), 0, LANGS), jax.random.fold_in(arg_keys[3], 1), 0, LANGS - 1).astype(jnp.int32)
    w_in = scatter_about(arg_keys[4], (FEAT, D), FEAT ** -0.5, 0.3125, ((1, 8),))
    lang_table = scatter_about(arg_keys[5], (LANGS, D), 0.5, 3.0, ((1, 8),))
    ln_gain = jnp.clip(1.0 + 0.18 * jax.random.normal(arg_keys[6], (D,), jnp.float32), 0.1, 1.9)
    w_pw1 = scatter_about(arg_keys[7], (D, 2, D), D ** -0.5, 0.15625, ((0, 64), (2, 8)))
    kernel = scatter_about(arg_keys[8], (KER, D), 0.3, 1.5, ((1, 8),), jnp.float32)
    bn_gain = jnp.clip(1.0 + 0.18 * jax.random.normal(arg_keys[9], (D,), jnp.float32), 0.1, 1.9)
    bn_bias = scatter_about(arg_keys[10], (D,), 0.5, 3.0, ((0, 8),), jnp.float32)
    w_pw2 = scatter_about(arg_keys[11], (D, D), D ** -0.5, 0.15625, ((0, 64), (1, 8)))
    cotangent = scatter_about(arg_keys[12], (TOTAL_ROWS, D), 1.0, 6.0, ((0, 64), (1, 8)))
    return {"corpus": corpus, "picks": picks, "lengths": lengths, "langs": langs, "w_in": w_in, "lang_table": lang_table, "ln_gain": ln_gain, "w_pw1": w_pw1, "kernel": kernel, "bn_gain": bn_gain, "bn_bias": bn_bias, "w_pw2": w_pw2, "cotangent": cotangent}


EPS = 1e-05

def depth_conv(values, taps):
    frames = BLK
    chans = values.shape[1]
    shaped = values.reshape(-1, frames, chans)
    margin = KER // 2
    padded = jnp.pad(shaped, ((0, 0), (margin, margin), (0, 0)))
    total = jnp.zeros(shaped.shape, jnp.float32)
    for step in range(KER):
        total = total + taps[step] * padded[:, step:step + frames]
    return total.reshape(values.shape)

def depth_back(grads, taps):
    frames = BLK
    chans = grads.shape[1]
    shaped = grads.reshape(-1, frames, chans)
    margin = KER // 2
    padded = jnp.pad(shaped, ((0, 0), (margin, margin), (0, 0)))
    total = jnp.zeros(shaped.shape, jnp.float32)
    for step in range(KER):
        begin = 2 * margin - step
        total = total + taps[step] * padded[:, begin:begin + frames]
    return total.reshape(grads.shape)

def kernel_terms(grads, values):
    frames = BLK
    chans = values.shape[1]
    shaped = values.reshape(-1, frames, chans)
    grad_shaped = grads.reshape(-1, frames, chans)
    margin = KER // 2
    padded = jnp.pad(shaped, ((0, 0), (margin, margin), (0, 0)))
    rows_out = []
    for step in range(KER):
        rows_out.append(lax.optimization_barrier(jnp.sum(grad_shaped * padded[:, step:step + frames], axis=(0, 1))))
    return jnp.stack(rows_out, 0)

def reference(corpus, picks, lengths, langs, w_in, lang_table, ln_gain, w_pw1, kernel, bn_gain, bn_bias, w_pw2, cotangent):
    block_ids = (jnp.arange(N_DP, dtype=jnp.int32)[None, :] * CB + picks.T).astype(jnp.int32).reshape(-1)
    chosen = corpus[block_ids]
    lens = lengths[block_ids]
    lang = langs[block_ids]
    valid = (jnp.arange(BLK, dtype=jnp.int32)[None, :] < lens[:, None]).astype(jnp.float32).reshape(-1)
    mel = chosen.reshape(-1, FEAT) * valid[:, None].astype(jnp.bfloat16)
    onehot = (lang[:, None] == jnp.arange(LANGS, dtype=jnp.int32)[None, :]).astype(jnp.bfloat16)
    lang_rows = jnp.dot(onehot, lang_table, preferred_element_type=jnp.float32)
    inputs = jnp.dot(mel, w_in, preferred_element_type=jnp.float32) + jnp.repeat(lang_rows, BLK, axis=0)
    mean = lax.optimization_barrier(jnp.sum(inputs, 1)) / D
    var = lax.optimization_barrier(jnp.sum(inputs * inputs, 1)) / D - mean * mean
    normed_in = ((inputs - mean[:, None]) * lax.rsqrt(var + EPS)[:, None] * ln_gain).astype(jnp.bfloat16)
    pre = jnp.dot(normed_in, w_pw1.reshape(D, 2 * D), preferred_element_type=jnp.float32)
    linear_part = pre[:, :D]
    gate_part = pre[:, D:]
    gate_sig = jax.nn.sigmoid(gate_part)
    glu_out = linear_part * gate_sig * valid[:, None]
    conv_out = depth_conv(glu_out, kernel)
    count = jnp.sum(valid)
    mu_conv = lax.optimization_barrier(jnp.sum(valid[:, None] * conv_out, 0)) / count
    var_conv = lax.optimization_barrier(jnp.sum(valid[:, None] * conv_out * conv_out, 0)) / count - mu_conv * mu_conv
    inv_std = lax.rsqrt(var_conv + EPS)
    normed_conv = (conv_out - mu_conv) * inv_std
    act = normed_conv * bn_gain + bn_bias
    act_sig = jax.nn.sigmoid(act)
    hidden = (valid[:, None] * act * act_sig).astype(jnp.bfloat16)
    encoded = (inputs + jnp.dot(hidden, w_pw2, preferred_element_type=jnp.float32)).astype(jnp.bfloat16)
    grad_pw2 = jnp.dot(hidden.T, cotangent, preferred_element_type=jnp.float32)
    dhidden = jnp.dot(cotangent, w_pw2.T, preferred_element_type=jnp.float32)
    dact = dhidden * valid[:, None] * act_sig * (1.0 + act * (1.0 - act_sig))
    grad_bias = lax.optimization_barrier(jnp.sum(dact, 0))
    grad_gain = lax.optimization_barrier(jnp.sum(dact * normed_conv, 0))
    dconv = valid[:, None] * inv_std * bn_gain * (dact - grad_bias / count - normed_conv * grad_gain / count)
    grad_kernel = kernel_terms(dconv, glu_out)
    dglu = depth_back(dconv, kernel)
    dlin = dglu * valid[:, None] * gate_sig
    dgate = dglu * valid[:, None] * linear_part * gate_sig * (1.0 - gate_sig)
    dpre = jnp.concatenate([dlin, dgate], 1).astype(jnp.bfloat16)
    grad_pw1 = jnp.dot(normed_in.T, dpre, preferred_element_type=jnp.float32).reshape(D, 2, D)
    return (encoded, grad_pw1, grad_pw2, grad_kernel, grad_gain, grad_bias)
```

```python
import jax
import jax.numpy as jnp
from jax import lax
from jax.sharding import Mesh, PartitionSpec as P

EPS = 1e-05


def depth_conv(values, taps, frames):
    chans = values.shape[1]
    shaped = values.reshape(-1, frames, chans)
    margin = taps.shape[0] // 2
    padded = jnp.pad(shaped, ((0, 0), (margin, margin), (0, 0)))
    total = jnp.zeros(shaped.shape, jnp.float32)
    for step in range(taps.shape[0]):
        total = total + taps[step] * padded[:, step : step + frames]
    return total.reshape(values.shape)


def depth_back(grads, taps, frames):
    chans = grads.shape[1]
    shaped = grads.reshape(-1, frames, chans)
    margin = taps.shape[0] // 2
    padded = jnp.pad(shaped, ((0, 0), (margin, margin), (0, 0)))
    total = jnp.zeros(shaped.shape, jnp.float32)
    for step in range(taps.shape[0]):
        begin = 2 * margin - step
        total = total + taps[step] * padded[:, begin : begin + frames]
    return total.reshape(grads.shape)


def kernel_terms(grads, values, width, frames):
    chans = values.shape[1]
    shaped = values.reshape(-1, frames, chans)
    grad_shaped = grads.reshape(-1, frames, chans)
    margin = width // 2
    padded = jnp.pad(shaped, ((0, 0), (margin, margin), (0, 0)))
    rows_out = []
    for step in range(width):
        rows_out.append(jnp.sum(grad_shaped * padded[:, step : step + frames], axis=(0, 1)))
    return jnp.stack(rows_out, 0)


DP_AXES = ("x", "y", "c")


def dp_sum(value):
    for name in reversed(DP_AXES):
        value = lax.psum(value, name)
    return value


def contract_rows(left, right):
    return lax.dot_general(
        left, right, (((0,), (0,)), ((), ())), preferred_element_type=jnp.float32
    )


def on_device(
    corpus,
    picks,
    lengths,
    langs,
    w_in,
    lang_table,
    ln_gain,
    w_pw1,
    kernel,
    bn_gain,
    bn_bias,
    w_pw2,
    cotangent,
):
    model_width = w_pw2.shape[0] * lax.axis_size(DP_AXES)
    chosen = picks[0]
    blocks = jnp.take(corpus, chosen, axis=0)
    lens_send = jnp.take(lengths, chosen)
    lang_send = jnp.take(langs, chosen)
    received, lens, lang = (
        lax.all_to_all(blocks, DP_AXES, split_axis=0, concat_axis=0, tiled=True),
        lax.all_to_all(lens_send, DP_AXES, split_axis=0, concat_axis=0, tiled=True),
        lax.all_to_all(lang_send, DP_AXES, split_axis=0, concat_axis=0, tiled=True),
    )
    frames = received.shape[1]
    valid = (
        (jnp.arange(frames, dtype=jnp.int32)[None, :] < lens[:, None])
        .astype(jnp.float32)
        .reshape(-1)
    )
    valid_col = valid[:, None]
    mel = received.reshape(-1, received.shape[2]) * valid_col.astype(jnp.bfloat16)
    onehot = (lang[:, None] == jnp.arange(lang_table.shape[0], dtype=jnp.int32)[None, :]).astype(
        jnp.bfloat16
    )
    lang_rows = jnp.dot(onehot, lang_table, preferred_element_type=jnp.float32)
    inputs = jnp.dot(mel, w_in, preferred_element_type=jnp.float32) + jnp.repeat(
        lang_rows, frames, axis=0
    )
    row_sum, row_sq = lax.psum((jnp.sum(inputs, 1), jnp.sum(inputs * inputs, 1)), "mp")
    mean = row_sum / model_width
    var = row_sq / model_width - mean * mean
    normed_in = ((inputs - mean[:, None]) * lax.rsqrt(var + EPS)[:, None] * ln_gain).astype(
        jnp.bfloat16
    )
    weights_one = lax.all_gather(w_pw1, DP_AXES, axis=0, tiled=True).reshape(model_width, -1)
    half = weights_one.shape[1] // 2
    normed_full = lax.all_gather(normed_in, "mp", axis=1, tiled=True)
    pre = jnp.dot(normed_full, weights_one, preferred_element_type=jnp.float32)
    linear_part = pre[:, :half]
    gate_part = pre[:, half:]
    gate_sig = jax.nn.sigmoid(gate_part)
    glu_out = linear_part * gate_sig * valid_col
    conv_out = depth_conv(glu_out, kernel, frames)
    sum_conv, sum_sq, count = dp_sum(
        (
            jnp.sum(valid_col * conv_out, 0),
            jnp.sum(valid_col * conv_out * conv_out, 0),
            jnp.sum(valid),
        )
    )
    mu_conv = sum_conv / count
    var_conv = sum_sq / count - mu_conv * mu_conv
    inv_std = lax.rsqrt(var_conv + EPS)
    normed_conv = (conv_out - mu_conv) * inv_std
    act = normed_conv * bn_gain + bn_bias
    act_sig = jax.nn.sigmoid(act)
    hidden = (valid_col * act * act_sig).astype(jnp.bfloat16)
    weights_two = lax.all_gather(w_pw2, DP_AXES, axis=0, tiled=True)
    hidden_full = lax.all_gather(hidden, "mp", axis=1, tiled=True)
    encoded = (
        inputs + jnp.dot(hidden_full, weights_two, preferred_element_type=jnp.float32)
    ).astype(jnp.bfloat16)
    grad_pw2 = lax.psum_scatter(
        contract_rows(hidden_full, cotangent), DP_AXES, scatter_dimension=0, tiled=True
    )
    cot_full = lax.all_gather(cotangent, "mp", axis=1, tiled=True)
    weights_rows = lax.all_to_all(weights_two, "mp", split_axis=0, concat_axis=1, tiled=True)
    dhidden = lax.dot_general(
        cot_full, weights_rows, (((1,), (1,)), ((), ())), preferred_element_type=jnp.float32
    )
    dact = dhidden * valid_col * act_sig * (1.0 + act * (1.0 - act_sig))
    grad_bias, grad_gain = dp_sum((jnp.sum(dact, 0), jnp.sum(dact * normed_conv, 0)))
    dconv = (
        valid_col * inv_std * bn_gain * (dact - grad_bias / count - normed_conv * grad_gain / count)
    )
    grad_kernel = dp_sum(kernel_terms(dconv, glu_out, kernel.shape[0], frames))
    dglu = depth_back(dconv, kernel, frames)
    dlin = dglu * valid_col * gate_sig
    dgate = dglu * valid_col * linear_part * gate_sig * (1.0 - gate_sig)
    dpre = jnp.concatenate([dlin, dgate], 1).astype(jnp.bfloat16)
    grad_pw1 = lax.psum_scatter(
        contract_rows(normed_full, dpre), DP_AXES, scatter_dimension=0, tiled=True
    )
    grad_pw1 = grad_pw1.reshape(grad_pw1.shape[0], 2, half)
    return (encoded, grad_pw1, grad_pw2, grad_kernel, grad_gain, grad_bias)


def dp_shape(mesh):
    along = mesh.devices[:, 0]
    try:
        xs = len({d.coords[0] for d in along})
        ys = len({d.coords[1] for d in along})
    except AttributeError:
        xs, ys = 1, 1
    cores = mesh.shape["dp"] // (xs * ys)
    return xs, ys, cores


def solution(mesh):
    xs, ys, cores = dp_shape(mesh)
    fine = Mesh(
        mesh.devices.reshape(xs, ys, cores, mesh.shape["mp"]), DP_AXES + ("mp",)
    )
    D = DP_AXES
    return jax.shard_map(
        on_device,
        mesh=fine,
        in_specs=(
            P(D, None, None),
            P(D, None),
            P(D),
            P(D),
            P(None, "mp"),
            P(None, "mp"),
            P("mp"),
            P(D, None, "mp"),
            P(None, "mp"),
            P("mp"),
            P("mp"),
            P(D, "mp"),
            P(D, "mp"),
        ),
        out_specs=(
            P(D, "mp"),
            P(D, None, "mp"),
            P(D, "mp"),
            P(None, "mp"),
            P("mp"),
            P("mp"),
        ),
        check_vma=False,
    )
```

```python
import jax
import jax.numpy as jnp
from jax import lax
from jax.sharding import Mesh, PartitionSpec as P

EPS = 1e-05


def depth_conv(values, taps, frames):
    chans = values.shape[1]
    shaped = values.reshape(-1, frames, chans)
    margin = taps.shape[0] // 2
    padded = jnp.pad(shaped, ((0, 0), (margin, margin), (0, 0)))
    total = jnp.zeros(shaped.shape, jnp.float32)
    for step in range(taps.shape[0]):
        total = total + taps[step] * padded[:, step : step + frames]
    return total.reshape(values.shape)


def depth_back(grads, taps, frames):
    chans = grads.shape[1]
    shaped = grads.reshape(-1, frames, chans)
    margin = taps.shape[0] // 2
    padded = jnp.pad(shaped, ((0, 0), (margin, margin), (0, 0)))
    total = jnp.zeros(shaped.shape, jnp.float32)
    for step in range(taps.shape[0]):
        begin = 2 * margin - step
        total = total + taps[step] * padded[:, begin : begin + frames]
    return total.reshape(grads.shape)


def kernel_terms(grads, values, width, frames):
    chans = values.shape[1]
    shaped = values.reshape(-1, frames, chans)
    grad_shaped = grads.reshape(-1, frames, chans)
    margin = width // 2
    padded = jnp.pad(shaped, ((0, 0), (margin, margin), (0, 0)))
    rows_out = []
    for step in range(width):
        rows_out.append(jnp.sum(grad_shaped * padded[:, step : step + frames], axis=(0, 1)))
    return jnp.stack(rows_out, 0)


DP_AXES = ("x", "y", "c")


def dp_sum(value):
    for name in reversed(DP_AXES):
        value = lax.psum(value, name)
    return value


def dp_gather(value):
    for name in reversed(DP_AXES):
        value = lax.all_gather(value, name, axis=0, tiled=True)
    return value


def dp_scatter(value):
    for name in DP_AXES:
        value = lax.psum_scatter(value, name, scatter_dimension=0, tiled=True)
    return value


def halving_scatter(value, sizes):
    cols = value.shape[1:]
    cur = value.reshape(tuple(sizes[a] for a in DP_AXES) + (-1,) + cols)
    for dim, name in reversed(list(enumerate(DP_AXES))):
        length = sizes[name]
        me = lax.axis_index(name)
        bit = length.bit_length() - 2
        while bit >= 0:
            shape = cur.shape
            span = shape[dim]
            split = shape[:dim] + (span >> (bit + 1), 2, 1 << bit) + shape[dim + 1 :]
            pieces = cur.reshape(split)
            mine = (me >> bit) & 1
            keep = lax.dynamic_index_in_dim(pieces, mine, dim + 1, keepdims=False)
            send = lax.dynamic_index_in_dim(pieces, 1 - mine, dim + 1, keepdims=False)
            perm = [(i, i ^ (1 << bit)) for i in range(length)]
            got = lax.ppermute(send, name, perm)
            merged = keep + got
            cur = merged.reshape(shape[:dim] + (span // 2,) + shape[dim + 1 :])
            bit -= 1
    return cur.reshape((-1,) + cols)


def contract_rows(left, right):
    return lax.dot_general(
        left, right, (((0,), (0,)), ((), ())), preferred_element_type=jnp.float32
    )


def on_device(
    corpus,
    picks,
    lengths,
    langs,
    w_in,
    lang_table,
    ln_gain,
    w_pw1,
    kernel,
    bn_gain,
    bn_bias,
    w_pw2,
    cotangent,
):
    model_width = w_pw2.shape[0] * lax.axis_size(DP_AXES)
    chosen = picks[0]
    blocks = jnp.take(corpus, chosen, axis=0)
    lens_send = jnp.take(lengths, chosen)
    lang_send = jnp.take(langs, chosen)
    received, lens, lang = (
        lax.all_to_all(blocks, DP_AXES, split_axis=0, concat_axis=0, tiled=True),
        lax.all_to_all(lens_send, DP_AXES, split_axis=0, concat_axis=0, tiled=True),
        lax.all_to_all(lang_send, DP_AXES, split_axis=0, concat_axis=0, tiled=True),
    )
    frames = received.shape[1]
    valid = (
        (jnp.arange(frames, dtype=jnp.int32)[None, :] < lens[:, None])
        .astype(jnp.float32)
        .reshape(-1)
    )
    valid_col = valid[:, None]
    mel = received.reshape(-1, received.shape[2]) * valid_col.astype(jnp.bfloat16)
    onehot = (lang[:, None] == jnp.arange(lang_table.shape[0], dtype=jnp.int32)[None, :]).astype(
        jnp.bfloat16
    )
    lang_rows = jnp.dot(onehot, lang_table, preferred_element_type=jnp.float32)
    inputs = jnp.dot(mel, w_in, preferred_element_type=jnp.float32) + jnp.repeat(
        lang_rows, frames, axis=0
    )
    row_sum, row_sq = lax.psum((jnp.sum(inputs, 1), jnp.sum(inputs * inputs, 1)), "mp")
    mean = row_sum / model_width
    var = row_sq / model_width - mean * mean
    normed_in = ((inputs - mean[:, None]) * lax.rsqrt(var + EPS)[:, None] * ln_gain).astype(
        jnp.bfloat16
    )
    weights_one = dp_gather(w_pw1).reshape(model_width, -1)
    half = weights_one.shape[1] // 2
    normed_full = lax.all_gather(normed_in, "mp", axis=1, tiled=True)
    pre = jnp.dot(normed_full, weights_one, preferred_element_type=jnp.float32)
    linear_part = pre[:, :half]
    gate_part = pre[:, half:]
    gate_sig = jax.nn.sigmoid(gate_part)
    glu_out = linear_part * gate_sig * valid_col
    conv_out = depth_conv(glu_out, kernel, frames)
    sum_conv, sum_sq, count = dp_sum(
        (
            jnp.sum(valid_col * conv_out, 0),
            jnp.sum(valid_col * conv_out * conv_out, 0),
            jnp.sum(valid),
        )
    )
    mu_conv = sum_conv / count
    var_conv = sum_sq / count - mu_conv * mu_conv
    inv_std = lax.rsqrt(var_conv + EPS)
    normed_conv = (conv_out - mu_conv) * inv_std
    act = normed_conv * bn_gain + bn_bias
    act_sig = jax.nn.sigmoid(act)
    hidden = (valid_col * act * act_sig).astype(jnp.bfloat16)
    weights_two = dp_gather(w_pw2)
    hidden_full = lax.all_gather(hidden, "mp", axis=1, tiled=True)
    encoded = (
        inputs + jnp.dot(hidden_full, weights_two, preferred_element_type=jnp.float32)
    ).astype(jnp.bfloat16)
    grad_pw2 = dp_scatter(contract_rows(hidden_full, cotangent))
    cot_full = lax.all_gather(cotangent, "mp", axis=1, tiled=True)
    weights_rows = lax.all_to_all(weights_two, "mp", split_axis=0, concat_axis=1, tiled=True)
    dhidden = lax.dot_general(
        cot_full, weights_rows, (((1,), (1,)), ((), ())), preferred_element_type=jnp.float32
    )
    dact = dhidden * valid_col * act_sig * (1.0 + act * (1.0 - act_sig))
    width = kernel.shape[0]
    term_a = kernel_terms(valid_col * dact, glu_out, width, frames)
    term_b = kernel_terms(jnp.broadcast_to(valid_col, glu_out.shape), glu_out, width, frames)
    term_e = kernel_terms(valid_col * normed_conv, glu_out, width, frames)
    grad_bias, grad_gain, term_a, term_b, term_e = dp_sum(
        (jnp.sum(dact, 0), jnp.sum(dact * normed_conv, 0), term_a, term_b, term_e)
    )
    scale = inv_std * bn_gain
    dconv = valid_col * scale * (dact - grad_bias / count - normed_conv * grad_gain / count)
    grad_kernel = scale * (term_a - (grad_bias / count) * term_b - (grad_gain / count) * term_e)
    dglu = depth_back(dconv, kernel, frames)
    dlin = dglu * valid_col * gate_sig
    dgate = dglu * valid_col * linear_part * gate_sig * (1.0 - gate_sig)
    dpre = jnp.concatenate([dlin, dgate], 1).astype(jnp.bfloat16)
    sizes = {name: lax.axis_size(name) for name in DP_AXES}
    grad_pw1 = halving_scatter(contract_rows(normed_full, dpre), sizes)
    grad_pw1 = grad_pw1.reshape(grad_pw1.shape[0], 2, half)
    return (encoded, grad_pw1, grad_pw2, grad_kernel, grad_gain, grad_bias)


def dp_shape(mesh):
    along = mesh.devices[:, 0]
    try:
        xs = len({d.coords[0] for d in along})
        ys = len({d.coords[1] for d in along})
    except AttributeError:
        xs, ys = 1, 1
    cores = mesh.shape["dp"] // (xs * ys)
    return xs, ys, cores


def solution(mesh):
    xs, ys, cores = dp_shape(mesh)
    fine = Mesh(
        mesh.devices.reshape(xs, ys, cores, mesh.shape["mp"]), DP_AXES + ("mp",)
    )
    D = DP_AXES
    return jax.shard_map(
        on_device,
        mesh=fine,
        in_specs=(
            P(D, None, None),
            P(D, None),
            P(D),
            P(D),
            P(None, "mp"),
            P(None, "mp"),
            P("mp"),
            P(D, None, "mp"),
            P(None, "mp"),
            P("mp"),
            P("mp"),
            P(D, "mp"),
            P(D, "mp"),
        ),
        out_specs=(
            P(D, "mp"),
            P(D, None, "mp"),
            P(D, "mp"),
            P(None, "mp"),
            P("mp"),
            P("mp"),
        ),
        check_vma=False,
    )
```

```python
import jax
import jax.numpy as jnp
from jax import lax
from jax.sharding import Mesh, PartitionSpec as P

EPS = 1e-05


def depth_conv(values, taps, frames):
    chans = values.shape[1]
    shaped = values.reshape(-1, frames, chans)
    margin = taps.shape[0] // 2
    padded = jnp.pad(shaped, ((0, 0), (margin, margin), (0, 0)))
    total = jnp.zeros(shaped.shape, jnp.float32)
    for step in range(taps.shape[0]):
        total = total + taps[step] * padded[:, step : step + frames]
    return total.reshape(values.shape)


def depth_back(grads, taps, frames):
    chans = grads.shape[1]
    shaped = grads.reshape(-1, frames, chans)
    margin = taps.shape[0] // 2
    padded = jnp.pad(shaped, ((0, 0), (margin, margin), (0, 0)))
    total = jnp.zeros(shaped.shape, jnp.float32)
    for step in range(taps.shape[0]):
        begin = 2 * margin - step
        total = total + taps[step] * padded[:, begin : begin + frames]
    return total.reshape(grads.shape)


def kernel_terms(grads, values, width, frames):
    chans = values.shape[1]
    shaped = values.reshape(-1, frames, chans)
    grad_shaped = grads.reshape(-1, frames, chans)
    margin = width // 2
    padded = jnp.pad(shaped, ((0, 0), (margin, margin), (0, 0)))
    rows_out = []
    for step in range(width):
        rows_out.append(jnp.sum(grad_shaped * padded[:, step : step + frames], axis=(0, 1)))
    return jnp.stack(rows_out, 0)


DP_AXES = ("x", "y", "c")


def dp_sum(value):
    for name in reversed(DP_AXES):
        value = lax.psum(value, name)
    return value


def dp_gather(value):
    for name in reversed(DP_AXES):
        value = lax.all_gather(value, name, axis=0, tiled=True)
    return value


def dp_scatter(value):
    for name in DP_AXES:
        value = lax.psum_scatter(value, name, scatter_dimension=0, tiled=True)
    return value


def halving_scatter(value, sizes):
    cols = value.shape[1:]
    cur = value.reshape(tuple(sizes[a] for a in DP_AXES) + (-1,) + cols)
    for dim, name in reversed(list(enumerate(DP_AXES))):
        length = sizes[name]
        me = lax.axis_index(name)
        bit = length.bit_length() - 2
        while bit >= 0:
            shape = cur.shape
            span = shape[dim]
            split = shape[:dim] + (span >> (bit + 1), 2, 1 << bit) + shape[dim + 1 :]
            pieces = cur.reshape(split)
            mine = (me >> bit) & 1
            keep = lax.dynamic_index_in_dim(pieces, mine, dim + 1, keepdims=False)
            send = lax.dynamic_index_in_dim(pieces, 1 - mine, dim + 1, keepdims=False)
            perm = [(i, i ^ (1 << bit)) for i in range(length)]
            got = lax.ppermute(send, name, perm)
            merged = keep + got
            cur = merged.reshape(shape[:dim] + (span // 2,) + shape[dim + 1 :])
            bit -= 1
    return cur.reshape((-1,) + cols)


def contract_rows(left, right):
    return lax.dot_general(
        left, right, (((0,), (0,)), ((), ())), preferred_element_type=jnp.float32
    )


def on_device(
    corpus,
    picks,
    lengths,
    langs,
    w_in,
    lang_table,
    ln_gain,
    w_pw1,
    kernel,
    bn_gain,
    bn_bias,
    w_pw2,
    cotangent,
):
    model_width = w_pw2.shape[0] * lax.axis_size(DP_AXES)
    chosen = picks[0]
    blocks = jnp.take(corpus, chosen, axis=0)
    meta_send = jnp.stack([jnp.take(lengths, chosen), jnp.take(langs, chosen)], 1)
    received = lax.all_to_all(blocks, DP_AXES, split_axis=0, concat_axis=0, tiled=True)
    meta = lax.all_to_all(meta_send, DP_AXES, split_axis=0, concat_axis=0, tiled=True)
    lens, lang = meta[:, 0], meta[:, 1]
    stacked = lax.all_gather(
        jnp.concatenate([w_pw1, w_pw2[:, None, :]], 1), DP_AXES, axis=0, tiled=True
    )
    frames = received.shape[1]
    valid = (
        (jnp.arange(frames, dtype=jnp.int32)[None, :] < lens[:, None])
        .astype(jnp.float32)
        .reshape(-1)
    )
    valid_col = valid[:, None]
    mel = received.reshape(-1, received.shape[2]) * valid_col.astype(jnp.bfloat16)
    onehot = (lang[:, None] == jnp.arange(lang_table.shape[0], dtype=jnp.int32)[None, :]).astype(
        jnp.bfloat16
    )
    lang_rows = jnp.dot(onehot, lang_table, preferred_element_type=jnp.float32)
    inputs = jnp.dot(mel, w_in, preferred_element_type=jnp.float32) + jnp.repeat(
        lang_rows, frames, axis=0
    )
    row_sum, row_sq = lax.psum((jnp.sum(inputs, 1), jnp.sum(inputs * inputs, 1)), "mp")
    mean = row_sum / model_width
    var = row_sq / model_width - mean * mean
    normed_in = ((inputs - mean[:, None]) * lax.rsqrt(var + EPS)[:, None] * ln_gain).astype(
        jnp.bfloat16
    )
    weights_one = stacked[:, :2].reshape(model_width, -1)
    half = weights_one.shape[1] // 2
    normed_full = lax.all_gather(normed_in, "mp", axis=1, tiled=True)
    pre = jnp.dot(normed_full, weights_one, preferred_element_type=jnp.float32)
    linear_part = pre[:, :half]
    gate_part = pre[:, half:]
    gate_sig = jax.nn.sigmoid(gate_part)
    glu_out = linear_part * gate_sig * valid_col
    conv_out = depth_conv(glu_out, kernel, frames)
    sum_conv, sum_sq, count = dp_sum(
        (
            jnp.sum(valid_col * conv_out, 0),
            jnp.sum(valid_col * conv_out * conv_out, 0),
            jnp.sum(valid),
        )
    )
    mu_conv = sum_conv / count
    var_conv = sum_sq / count - mu_conv * mu_conv
    inv_std = lax.rsqrt(var_conv + EPS)
    normed_conv = (conv_out - mu_conv) * inv_std
    act = normed_conv * bn_gain + bn_bias
    act_sig = jax.nn.sigmoid(act)
    hidden = (valid_col * act * act_sig).astype(jnp.bfloat16)
    weights_two = stacked[:, 2]
    hidden_full = lax.all_gather(hidden, "mp", axis=1, tiled=True)
    encoded = (
        inputs + jnp.dot(hidden_full, weights_two, preferred_element_type=jnp.float32)
    ).astype(jnp.bfloat16)
    grad_pw2 = dp_scatter(contract_rows(hidden_full, cotangent))
    cot_full = lax.all_gather(cotangent, "mp", axis=1, tiled=True)
    weights_rows = lax.all_to_all(weights_two, "mp", split_axis=0, concat_axis=1, tiled=True)
    dhidden = lax.dot_general(
        cot_full, weights_rows, (((1,), (1,)), ((), ())), preferred_element_type=jnp.float32
    )
    dact = dhidden * valid_col * act_sig * (1.0 + act * (1.0 - act_sig))
    grad_bias, grad_gain = dp_sum((jnp.sum(dact, 0), jnp.sum(dact * normed_conv, 0)))
    dconv = (
        valid_col * inv_std * bn_gain * (dact - grad_bias / count - normed_conv * grad_gain / count)
    )
    grad_kernel = dp_sum(kernel_terms(dconv, glu_out, kernel.shape[0], frames))
    dglu = depth_back(dconv, kernel, frames)
    dlin = dglu * valid_col * gate_sig
    dgate = dglu * valid_col * linear_part * gate_sig * (1.0 - gate_sig)
    dpre = jnp.concatenate([dlin, dgate], 1).astype(jnp.bfloat16)
    sizes = {name: lax.axis_size(name) for name in DP_AXES}
    grad_pw1 = halving_scatter(contract_rows(normed_full, dpre), sizes)
    grad_pw1 = grad_pw1.reshape(grad_pw1.shape[0], 2, half)
    return (encoded, grad_pw1, grad_pw2, grad_kernel, grad_gain, grad_bias)


def dp_shape(mesh):
    along = mesh.devices[:, 0]
    try:
        xs = len({d.coords[0] for d in along})
        ys = len({d.coords[1] for d in along})
    except AttributeError:
        xs, ys = 1, 1
    cores = mesh.shape["dp"] // (xs * ys)
    return xs, ys, cores


def solution(mesh):
    xs, ys, cores = dp_shape(mesh)
    fine = Mesh(
        mesh.devices.reshape(xs, ys, cores, mesh.shape["mp"]), DP_AXES + ("mp",)
    )
    D = DP_AXES
    return jax.shard_map(
        on_device,
        mesh=fine,
        in_specs=(
            P(D, None, None),
            P(D, None),
            P(D),
            P(D),
            P(None, "mp"),
            P(None, "mp"),
            P("mp"),
            P(D, None, "mp"),
            P(None, "mp"),
            P("mp"),
            P("mp"),
            P(D, "mp"),
            P(D, "mp"),
        ),
        out_specs=(
            P(D, "mp"),
            P(D, None, "mp"),
            P(D, "mp"),
            P(None, "mp"),
            P("mp"),
            P("mp"),
        ),
        check_vma=False,
    )
```

```python
import jax
import jax.numpy as jnp
from jax import lax
from jax.sharding import Mesh, PartitionSpec as P

EPS = 1e-05


def depth_conv(values, taps, frames):
    chans = values.shape[1]
    shaped = values.reshape(-1, frames, chans)
    margin = taps.shape[0] // 2
    padded = jnp.pad(shaped, ((0, 0), (margin, margin), (0, 0)))
    total = jnp.zeros(shaped.shape, jnp.float32)
    for step in range(taps.shape[0]):
        total = total + taps[step] * padded[:, step : step + frames]
    return total.reshape(values.shape)


def depth_back(grads, taps, frames):
    chans = grads.shape[1]
    shaped = grads.reshape(-1, frames, chans)
    margin = taps.shape[0] // 2
    padded = jnp.pad(shaped, ((0, 0), (margin, margin), (0, 0)))
    total = jnp.zeros(shaped.shape, jnp.float32)
    for step in range(taps.shape[0]):
        begin = 2 * margin - step
        total = total + taps[step] * padded[:, begin : begin + frames]
    return total.reshape(grads.shape)


def kernel_terms(grads, values, width, frames):
    chans = values.shape[1]
    shaped = values.reshape(-1, frames, chans)
    grad_shaped = grads.reshape(-1, frames, chans)
    margin = width // 2
    padded = jnp.pad(shaped, ((0, 0), (margin, margin), (0, 0)))
    rows_out = []
    for step in range(width):
        rows_out.append(jnp.sum(grad_shaped * padded[:, step : step + frames], axis=(0, 1)))
    return jnp.stack(rows_out, 0)


DP_AXES = ("x", "y", "c")


def dp_sum(value):
    for name in reversed(DP_AXES):
        value = lax.psum(value, name)
    return value


def dp_gather(value):
    for name in reversed(DP_AXES):
        value = lax.all_gather(value, name, axis=0, tiled=True)
    return value


def dp_scatter(value):
    for name in DP_AXES:
        value = lax.psum_scatter(value, name, scatter_dimension=0, tiled=True)
    return value


def halving_scatter(value, sizes):
    cols = value.shape[1:]
    cur = value.reshape(tuple(sizes[a] for a in DP_AXES) + (-1,) + cols)
    for dim, name in reversed(list(enumerate(DP_AXES))):
        length = sizes[name]
        me = lax.axis_index(name)
        bit = length.bit_length() - 2
        while bit >= 0:
            shape = cur.shape
            span = shape[dim]
            split = shape[:dim] + (span >> (bit + 1), 2, 1 << bit) + shape[dim + 1 :]
            pieces = cur.reshape(split)
            mine = (me >> bit) & 1
            keep = lax.dynamic_index_in_dim(pieces, mine, dim + 1, keepdims=False)
            send = lax.dynamic_index_in_dim(pieces, 1 - mine, dim + 1, keepdims=False)
            perm = [(i, i ^ (1 << bit)) for i in range(length)]
            got = lax.ppermute(send, name, perm)
            merged = keep + got
            cur = merged.reshape(shape[:dim] + (span // 2,) + shape[dim + 1 :])
            bit -= 1
    return cur.reshape((-1,) + cols)


def doubling_gather(value, name):
    length = lax.axis_size(name)
    me = lax.axis_index(name)
    cur = value[None]
    bit = 0
    while (1 << bit) < length:
        perm = [(i, i ^ (1 << bit)) for i in range(length)]
        got = lax.ppermute(cur, name, perm)
        low = ((me >> bit) & 1) == 0
        cur = jnp.where(low, jnp.concatenate([cur, got]), jnp.concatenate([got, cur]))
        bit += 1
    return cur


def contract_rows(left, right):
    return lax.dot_general(
        left, right, (((0,), (0,)), ((), ())), preferred_element_type=jnp.float32
    )


def on_device(
    corpus,
    picks,
    lengths,
    langs,
    w_in,
    lang_table,
    ln_gain,
    w_pw1,
    kernel,
    bn_gain,
    bn_bias,
    w_pw2,
    cotangent,
):
    model_width = w_pw2.shape[0] * lax.axis_size(DP_AXES)
    chosen = picks[0]
    blocks = jnp.take(corpus, chosen, axis=0)
    meta_send = jnp.stack([jnp.take(lengths, chosen), jnp.take(langs, chosen)], 1)
    received = lax.all_to_all(blocks, DP_AXES, split_axis=0, concat_axis=0, tiled=True)
    meta = lax.all_to_all(meta_send, DP_AXES, split_axis=0, concat_axis=0, tiled=True)
    lens, lang = meta[:, 0], meta[:, 1]
    stacked = lax.all_gather(
        jnp.concatenate([w_pw1, w_pw2[:, None, :]], 1), DP_AXES, axis=0, tiled=True
    )
    frames = received.shape[1]
    valid = (
        (jnp.arange(frames, dtype=jnp.int32)[None, :] < lens[:, None])
        .astype(jnp.float32)
        .reshape(-1)
    )
    valid_col = valid[:, None]
    mel = received.reshape(-1, received.shape[2]) * valid_col.astype(jnp.bfloat16)
    onehot = (lang[:, None] == jnp.arange(lang_table.shape[0], dtype=jnp.int32)[None, :]).astype(
        jnp.bfloat16
    )
    feats = w_in.shape[0]
    tables = doubling_gather(jnp.concatenate([w_in, lang_table], 0), "mp")
    gains = doubling_gather(ln_gain, "mp").reshape(-1)
    parts, _, cols = tables.shape
    tables = jnp.transpose(tables, (1, 0, 2)).reshape(-1, parts * cols)
    w_in_full, lang_full = tables[:feats], tables[feats:]
    lang_rows = jnp.dot(onehot, lang_full, preferred_element_type=jnp.float32)
    inputs_full = jnp.dot(mel, w_in_full, preferred_element_type=jnp.float32) + jnp.repeat(
        lang_rows, frames, axis=0
    )
    mean = jnp.sum(inputs_full, 1) / model_width
    var = jnp.sum(inputs_full * inputs_full, 1) / model_width - mean * mean
    normed_full = (
        (inputs_full - mean[:, None]) * lax.rsqrt(var + EPS)[:, None] * gains
    ).astype(jnp.bfloat16)
    inputs = lax.dynamic_slice_in_dim(inputs_full, lax.axis_index("mp") * cols, cols, 1)
    weights_one = stacked[:, :2].reshape(model_width, -1)
    half = weights_one.shape[1] // 2
    pre = jnp.dot(normed_full, weights_one, preferred_element_type=jnp.float32)
    linear_part = pre[:, :half]
    gate_part = pre[:, half:]
    gate_sig = jax.nn.sigmoid(gate_part)
    glu_out = linear_part * gate_sig * valid_col
    conv_out = depth_conv(glu_out, kernel, frames)
    sum_conv, sum_sq, count = dp_sum(
        (
            jnp.sum(valid_col * conv_out, 0),
            jnp.sum(valid_col * conv_out * conv_out, 0),
            jnp.sum(valid),
        )
    )
    mu_conv = sum_conv / count
    var_conv = sum_sq / count - mu_conv * mu_conv
    inv_std = lax.rsqrt(var_conv + EPS)
    normed_conv = (conv_out - mu_conv) * inv_std
    act = normed_conv * bn_gain + bn_bias
    act_sig = jax.nn.sigmoid(act)
    hidden = (valid_col * act * act_sig).astype(jnp.bfloat16)
    weights_two = stacked[:, 2]
    hidden_full = lax.all_gather(hidden, "mp", axis=1, tiled=True)
    encoded = (
        inputs + jnp.dot(hidden_full, weights_two, preferred_element_type=jnp.float32)
    ).astype(jnp.bfloat16)
    grad_pw2 = dp_scatter(contract_rows(hidden_full, cotangent))
    cot_full = lax.all_gather(cotangent, "mp", axis=1, tiled=True)
    weights_rows = lax.all_to_all(weights_two, "mp", split_axis=0, concat_axis=1, tiled=True)
    dhidden = lax.dot_general(
        cot_full, weights_rows, (((1,), (1,)), ((), ())), preferred_element_type=jnp.float32
    )
    dact = dhidden * valid_col * act_sig * (1.0 + act * (1.0 - act_sig))
    grad_bias, grad_gain = dp_sum((jnp.sum(dact, 0), jnp.sum(dact * normed_conv, 0)))
    dconv = (
        valid_col * inv_std * bn_gain * (dact - grad_bias / count - normed_conv * grad_gain / count)
    )
    grad_kernel = dp_sum(kernel_terms(dconv, glu_out, kernel.shape[0], frames))
    dglu = depth_back(dconv, kernel, frames)
    dlin = dglu * valid_col * gate_sig
    dgate = dglu * valid_col * linear_part * gate_sig * (1.0 - gate_sig)
    dpre = jnp.concatenate([dlin, dgate], 1).astype(jnp.bfloat16)
    sizes = {name: lax.axis_size(name) for name in DP_AXES}
    grad_pw1 = halving_scatter(contract_rows(normed_full, dpre), sizes)
    grad_pw1 = grad_pw1.reshape(grad_pw1.shape[0], 2, half)
    return (encoded, grad_pw1, grad_pw2, grad_kernel, grad_gain, grad_bias)


def dp_shape(mesh):
    along = mesh.devices[:, 0]
    try:
        xs = len({d.coords[0] for d in along})
        ys = len({d.coords[1] for d in along})
    except AttributeError:
        xs, ys = 1, 1
    cores = mesh.shape["dp"] // (xs * ys)
    return xs, ys, cores


def solution(mesh):
    xs, ys, cores = dp_shape(mesh)
    fine = Mesh(
        mesh.devices.reshape(xs, ys, cores, mesh.shape["mp"]), DP_AXES + ("mp",)
    )
    D = DP_AXES
    return jax.shard_map(
        on_device,
        mesh=fine,
        in_specs=(
            P(D, None, None),
            P(D, None),
            P(D),
            P(D),
            P(None, "mp"),
            P(None, "mp"),
            P("mp"),
            P(D, None, "mp"),
            P(None, "mp"),
            P("mp"),
            P("mp"),
            P(D, "mp"),
            P(D, "mp"),
        ),
        out_specs=(
            P(D, "mp"),
            P(D, None, "mp"),
            P(D, "mp"),
            P(None, "mp"),
            P("mp"),
            P("mp"),
        ),
        check_vma=False,
    )
```

```python
import jax
import jax.numpy as jnp
from jax import lax
from jax.sharding import Mesh, PartitionSpec as P

EPS = 1e-05


def depth_conv(values, taps, frames):
    chans = values.shape[1]
    shaped = values.reshape(-1, frames, chans)
    margin = taps.shape[0] // 2
    padded = jnp.pad(shaped, ((0, 0), (margin, margin), (0, 0)))
    total = jnp.zeros(shaped.shape, jnp.float32)
    for step in range(taps.shape[0]):
        total = total + taps[step] * padded[:, step : step + frames]
    return total.reshape(values.shape)


def depth_back(grads, taps, frames):
    chans = grads.shape[1]
    shaped = grads.reshape(-1, frames, chans)
    margin = taps.shape[0] // 2
    padded = jnp.pad(shaped, ((0, 0), (margin, margin), (0, 0)))
    total = jnp.zeros(shaped.shape, jnp.float32)
    for step in range(taps.shape[0]):
        begin = 2 * margin - step
        total = total + taps[step] * padded[:, begin : begin + frames]
    return total.reshape(grads.shape)


def kernel_terms(grads, values, width, frames):
    chans = values.shape[1]
    shaped = values.reshape(-1, frames, chans)
    grad_shaped = grads.reshape(-1, frames, chans)
    margin = width // 2
    padded = jnp.pad(shaped, ((0, 0), (margin, margin), (0, 0)))
    rows_out = []
    for step in range(width):
        rows_out.append(jnp.sum(grad_shaped * padded[:, step : step + frames], axis=(0, 1)))
    return jnp.stack(rows_out, 0)


DP_AXES = ("x", "y", "c")


def dp_sum(value):
    for name in reversed(DP_AXES):
        value = lax.psum(value, name)
    return value


def dp_gather(value):
    for name in reversed(DP_AXES):
        value = lax.all_gather(value, name, axis=0, tiled=True)
    return value


def dp_scatter(value):
    for name in DP_AXES:
        value = lax.psum_scatter(value, name, scatter_dimension=0, tiled=True)
    return value


def halving_scatter(value, sizes, extra):
    cols = value.shape[1:]
    cur = value.reshape(tuple(sizes[a] for a in DP_AXES) + (-1,) + cols)
    rows = extra.shape[0]
    for dim, name in reversed(list(enumerate(DP_AXES))):
        length = sizes[name]
        me = lax.axis_index(name)
        bit = length.bit_length() - 2
        while bit >= 0:
            shape = cur.shape
            span = shape[dim]
            split = shape[:dim] + (span >> (bit + 1), 2, 1 << bit) + shape[dim + 1 :]
            pieces = cur.reshape(split)
            mine = (me >> bit) & 1
            keep = lax.dynamic_index_in_dim(pieces, mine, dim + 1, keepdims=False)
            send = lax.dynamic_index_in_dim(pieces, 1 - mine, dim + 1, keepdims=False)
            perm = [(i, i ^ (1 << bit)) for i in range(length)]
            message = jnp.concatenate([send.reshape((-1,) + cols), extra], 0)
            got = lax.ppermute(message, name, perm)
            merged = keep + got[:-rows].reshape(send.shape)
            extra = extra + got[-rows:]
            cur = merged.reshape(shape[:dim] + (span // 2,) + shape[dim + 1 :])
            bit -= 1
    return cur.reshape((-1,) + cols), extra


def doubling_gather(value, name):
    length = lax.axis_size(name)
    me = lax.axis_index(name)
    cur = value[None]
    bit = 0
    while (1 << bit) < length:
        perm = [(i, i ^ (1 << bit)) for i in range(length)]
        got = lax.ppermute(cur, name, perm)
        low = ((me >> bit) & 1) == 0
        cur = jnp.where(low, jnp.concatenate([cur, got]), jnp.concatenate([got, cur]))
        bit += 1
    return cur


def contract_rows(left, right):
    return lax.dot_general(
        left, right, (((0,), (0,)), ((), ())), preferred_element_type=jnp.float32
    )


def on_device(
    corpus,
    picks,
    lengths,
    langs,
    w_in,
    lang_table,
    ln_gain,
    w_pw1,
    kernel,
    bn_gain,
    bn_bias,
    w_pw2,
    cotangent,
):
    model_width = w_pw2.shape[0] * lax.axis_size(DP_AXES)
    chosen = picks[0]
    blocks = jnp.take(corpus, chosen, axis=0)
    meta_send = jnp.stack([jnp.take(lengths, chosen), jnp.take(langs, chosen)], 1)
    received = lax.all_to_all(blocks, DP_AXES, split_axis=0, concat_axis=0, tiled=True)
    meta = lax.all_to_all(meta_send, DP_AXES, split_axis=0, concat_axis=0, tiled=True)
    lens, lang = meta[:, 0], meta[:, 1]
    stacked = lax.all_gather(
        jnp.concatenate([w_pw1, w_pw2[:, None, :]], 1), DP_AXES, axis=0, tiled=True
    )
    frames = received.shape[1]
    valid = (
        (jnp.arange(frames, dtype=jnp.int32)[None, :] < lens[:, None])
        .astype(jnp.float32)
        .reshape(-1)
    )
    valid_col = valid[:, None]
    mel = received.reshape(-1, received.shape[2]) * valid_col.astype(jnp.bfloat16)
    onehot = (lang[:, None] == jnp.arange(lang_table.shape[0], dtype=jnp.int32)[None, :]).astype(
        jnp.bfloat16
    )
    feats = w_in.shape[0]
    tables = doubling_gather(jnp.concatenate([w_in, lang_table], 0), "mp")
    gains = doubling_gather(ln_gain, "mp").reshape(-1)
    parts, _, cols = tables.shape
    tables = jnp.transpose(tables, (1, 0, 2)).reshape(-1, parts * cols)
    w_in_full, lang_full = tables[:feats], tables[feats:]
    lang_rows = jnp.dot(onehot, lang_full, preferred_element_type=jnp.float32)
    inputs_full = jnp.dot(mel, w_in_full, preferred_element_type=jnp.float32) + jnp.repeat(
        lang_rows, frames, axis=0
    )
    mean = jnp.sum(inputs_full, 1) / model_width
    var = jnp.sum(inputs_full * inputs_full, 1) / model_width - mean * mean
    normed_full = (
        (inputs_full - mean[:, None]) * lax.rsqrt(var + EPS)[:, None] * gains
    ).astype(jnp.bfloat16)
    inputs = lax.dynamic_slice_in_dim(inputs_full, lax.axis_index("mp") * cols, cols, 1)
    weights_one = stacked[:, :2].reshape(model_width, -1)
    half = weights_one.shape[1] // 2
    pre = jnp.dot(normed_full, weights_one, preferred_element_type=jnp.float32)
    linear_part = pre[:, :half]
    gate_part = pre[:, half:]
    gate_sig = jax.nn.sigmoid(gate_part)
    glu_out = linear_part * gate_sig * valid_col
    conv_out = depth_conv(glu_out, kernel, frames)
    sum_conv, sum_sq, count = dp_sum(
        (
            jnp.sum(valid_col * conv_out, 0),
            jnp.sum(valid_col * conv_out * conv_out, 0),
            jnp.sum(valid),
        )
    )
    mu_conv = sum_conv / count
    var_conv = sum_sq / count - mu_conv * mu_conv
    inv_std = lax.rsqrt(var_conv + EPS)
    normed_conv = (conv_out - mu_conv) * inv_std
    act = normed_conv * bn_gain + bn_bias
    act_sig = jax.nn.sigmoid(act)
    hidden = (valid_col * act * act_sig).astype(jnp.bfloat16)
    weights_two = stacked[:, 2]
    hidden_full = lax.all_gather(hidden, "mp", axis=1, tiled=True)
    encoded = (
        inputs + jnp.dot(hidden_full, weights_two, preferred_element_type=jnp.float32)
    ).astype(jnp.bfloat16)
    grad_pw2 = dp_scatter(contract_rows(hidden_full, cotangent))
    cot_full = lax.all_gather(cotangent, "mp", axis=1, tiled=True)
    weights_rows = lax.all_to_all(weights_two, "mp", split_axis=0, concat_axis=1, tiled=True)
    dhidden = lax.dot_general(
        cot_full, weights_rows, (((1,), (1,)), ((), ())), preferred_element_type=jnp.float32
    )
    dact = dhidden * valid_col * act_sig * (1.0 + act * (1.0 - act_sig))
    grad_bias, grad_gain = dp_sum((jnp.sum(dact, 0), jnp.sum(dact * normed_conv, 0)))
    dconv = (
        valid_col * inv_std * bn_gain * (dact - grad_bias / count - normed_conv * grad_gain / count)
    )
    kernel_part = kernel_terms(dconv, glu_out, kernel.shape[0], frames)
    dglu = depth_back(dconv, kernel, frames)
    dlin = dglu * valid_col * gate_sig
    dgate = dglu * valid_col * linear_part * gate_sig * (1.0 - gate_sig)
    dpre = jnp.concatenate([dlin, dgate], 1).astype(jnp.bfloat16)
    sizes = {name: lax.axis_size(name) for name in DP_AXES}
    width = dpre.shape[1]
    flat = kernel_part.reshape(-1)
    pad = (-flat.shape[0]) % width
    extra = jnp.pad(flat, (0, pad)).reshape(-1, width)
    grad_pw1, extra = halving_scatter(contract_rows(normed_full, dpre), sizes, extra)
    grad_kernel = extra.reshape(-1)[: flat.shape[0]].reshape(kernel_part.shape)
    grad_pw1 = grad_pw1.reshape(grad_pw1.shape[0], 2, half)
    return (encoded, grad_pw1, grad_pw2, grad_kernel, grad_gain, grad_bias)


def dp_shape(mesh):
    along = mesh.devices[:, 0]
    try:
        xs = len({d.coords[0] for d in along})
        ys = len({d.coords[1] for d in along})
    except AttributeError:
        xs, ys = 1, 1
    cores = mesh.shape["dp"] // (xs * ys)
    return xs, ys, cores


def solution(mesh):
    xs, ys, cores = dp_shape(mesh)
    fine = Mesh(
        mesh.devices.reshape(xs, ys, cores, mesh.shape["mp"]), DP_AXES + ("mp",)
    )
    D = DP_AXES
    return jax.shard_map(
        on_device,
        mesh=fine,
        in_specs=(
            P(D, None, None),
            P(D, None),
            P(D),
            P(D),
            P(None, "mp"),
            P(None, "mp"),
            P("mp"),
            P(D, None, "mp"),
            P(None, "mp"),
            P("mp"),
            P("mp"),
            P(D, "mp"),
            P(D, "mp"),
        ),
        out_specs=(
            P(D, "mp"),
            P(D, None, "mp"),
            P(D, "mp"),
            P(None, "mp"),
            P("mp"),
            P("mp"),
        ),
        check_vma=False,
    )
```

```python
import jax
import jax.numpy as jnp
from jax import lax
from jax.sharding import Mesh, PartitionSpec as P

EPS = 1e-05


def depth_conv(values, taps, frames):
    chans = values.shape[1]
    shaped = values.reshape(-1, frames, chans)
    margin = taps.shape[0] // 2
    padded = jnp.pad(shaped, ((0, 0), (margin, margin), (0, 0)))
    total = jnp.zeros(shaped.shape, jnp.float32)
    for step in range(taps.shape[0]):
        total = total + taps[step] * padded[:, step : step + frames]
    return total.reshape(values.shape)


def depth_back(grads, taps, frames):
    chans = grads.shape[1]
    shaped = grads.reshape(-1, frames, chans)
    margin = taps.shape[0] // 2
    padded = jnp.pad(shaped, ((0, 0), (margin, margin), (0, 0)))
    total = jnp.zeros(shaped.shape, jnp.float32)
    for step in range(taps.shape[0]):
        begin = 2 * margin - step
        total = total + taps[step] * padded[:, begin : begin + frames]
    return total.reshape(grads.shape)


def kernel_terms(grads, values, width, frames):
    chans = values.shape[1]
    shaped = values.reshape(-1, frames, chans)
    grad_shaped = grads.reshape(-1, frames, chans)
    margin = width // 2
    padded = jnp.pad(shaped, ((0, 0), (margin, margin), (0, 0)))
    rows_out = []
    for step in range(width):
        rows_out.append(jnp.sum(grad_shaped * padded[:, step : step + frames], axis=(0, 1)))
    return jnp.stack(rows_out, 0)


DP_AXES = ("x", "y", "c")


def dp_sum(value):
    for name in reversed(DP_AXES):
        value = lax.psum(value, name)
    return value


def dp_gather(value):
    for name in reversed(DP_AXES):
        value = lax.all_gather(value, name, axis=0, tiled=True)
    return value


def dp_scatter(value):
    for name in DP_AXES:
        value = lax.psum_scatter(value, name, scatter_dimension=0, tiled=True)
    return value


def halving_scatter(value, sizes, extra):
    cols = value.shape[1:]
    cur = value.reshape(tuple(sizes[a] for a in DP_AXES) + (-1,) + cols)
    rows = None if extra is None else extra.shape[0]
    for dim, name in reversed(list(enumerate(DP_AXES))):
        length = sizes[name]
        me = lax.axis_index(name)
        bit = length.bit_length() - 2
        while bit >= 0:
            shape = cur.shape
            span = shape[dim]
            split = shape[:dim] + (span >> (bit + 1), 2, 1 << bit) + shape[dim + 1 :]
            pieces = cur.reshape(split)
            mine = (me >> bit) & 1
            keep = lax.dynamic_index_in_dim(pieces, mine, dim + 1, keepdims=False)
            send = lax.dynamic_index_in_dim(pieces, 1 - mine, dim + 1, keepdims=False)
            perm = [(i, i ^ (1 << bit)) for i in range(length)]
            if extra is None:
                merged = keep + lax.ppermute(send, name, perm)
            else:
                message = jnp.concatenate([send.reshape((-1,) + cols), extra], 0)
                got = lax.ppermute(message, name, perm)
                merged = keep + got[:-rows].reshape(send.shape)
                extra = extra + got[-rows:]
            cur = merged.reshape(shape[:dim] + (span // 2,) + shape[dim + 1 :])
            bit -= 1
    return cur.reshape((-1,) + cols), extra


def doubling_gather(value, name):
    length = lax.axis_size(name)
    me = lax.axis_index(name)
    cur = value[None]
    bit = 0
    while (1 << bit) < length:
        perm = [(i, i ^ (1 << bit)) for i in range(length)]
        got = lax.ppermute(cur, name, perm)
        low = ((me >> bit) & 1) == 0
        cur = jnp.where(low, jnp.concatenate([cur, got]), jnp.concatenate([got, cur]))
        bit += 1
    return cur


def contract_rows(left, right):
    return lax.dot_general(
        left, right, (((0,), (0,)), ((), ())), preferred_element_type=jnp.float32
    )


def on_device(
    corpus,
    picks,
    lengths,
    langs,
    w_in,
    lang_table,
    ln_gain,
    w_pw1,
    kernel,
    bn_gain,
    bn_bias,
    w_pw2,
    cotangent,
):
    model_width = w_pw2.shape[0] * lax.axis_size(DP_AXES)
    chosen = picks[0]
    blocks = jnp.take(corpus, chosen, axis=0)
    meta_send = jnp.stack([jnp.take(lengths, chosen), jnp.take(langs, chosen)], 1)
    received = lax.all_to_all(blocks, DP_AXES, split_axis=0, concat_axis=0, tiled=True)
    meta = lax.all_to_all(meta_send, DP_AXES, split_axis=0, concat_axis=0, tiled=True)
    lens, lang = meta[:, 0], meta[:, 1]
    stacked = lax.all_gather(
        jnp.concatenate([w_pw1, w_pw2[:, None, :]], 1), DP_AXES, axis=0, tiled=True
    )
    frames = received.shape[1]
    valid = (
        (jnp.arange(frames, dtype=jnp.int32)[None, :] < lens[:, None])
        .astype(jnp.float32)
        .reshape(-1)
    )
    valid_col = valid[:, None]
    mel = received.reshape(-1, received.shape[2]) * valid_col.astype(jnp.bfloat16)
    onehot = (lang[:, None] == jnp.arange(lang_table.shape[0], dtype=jnp.int32)[None, :]).astype(
        jnp.bfloat16
    )
    feats = w_in.shape[0]
    tables = doubling_gather(jnp.concatenate([w_in, lang_table], 0), "mp")
    gains = doubling_gather(ln_gain, "mp").reshape(-1)
    parts, _, cols = tables.shape
    tables = jnp.transpose(tables, (1, 0, 2)).reshape(-1, parts * cols)
    w_in_full, lang_full = tables[:feats], tables[feats:]
    lang_rows = jnp.dot(onehot, lang_full, preferred_element_type=jnp.float32)
    inputs_full = jnp.dot(mel, w_in_full, preferred_element_type=jnp.float32) + jnp.repeat(
        lang_rows, frames, axis=0
    )
    mean = jnp.sum(inputs_full, 1) / model_width
    var = jnp.sum(inputs_full * inputs_full, 1) / model_width - mean * mean
    normed_full = (
        (inputs_full - mean[:, None]) * lax.rsqrt(var + EPS)[:, None] * gains
    ).astype(jnp.bfloat16)
    inputs = lax.dynamic_slice_in_dim(inputs_full, lax.axis_index("mp") * cols, cols, 1)
    weights_one = stacked[:, :2].reshape(model_width, -1)
    half = weights_one.shape[1] // 2
    pre = jnp.dot(normed_full, weights_one, preferred_element_type=jnp.float32)
    linear_part = pre[:, :half]
    gate_part = pre[:, half:]
    gate_sig = jax.nn.sigmoid(gate_part)
    glu_out = linear_part * gate_sig * valid_col
    conv_out = depth_conv(glu_out, kernel, frames)
    sum_conv, sum_sq, count = dp_sum(
        (
            jnp.sum(valid_col * conv_out, 0),
            jnp.sum(valid_col * conv_out * conv_out, 0),
            jnp.sum(valid),
        )
    )
    mu_conv = sum_conv / count
    var_conv = sum_sq / count - mu_conv * mu_conv
    inv_std = lax.rsqrt(var_conv + EPS)
    normed_conv = (conv_out - mu_conv) * inv_std
    act = normed_conv * bn_gain + bn_bias
    act_sig = jax.nn.sigmoid(act)
    hidden = (valid_col * act * act_sig).astype(jnp.bfloat16)
    weights_two = stacked[:, 2]
    hidden_full = lax.all_gather(hidden, "mp", axis=1, tiled=True)
    encoded = (
        inputs + jnp.dot(hidden_full, weights_two, preferred_element_type=jnp.float32)
    ).astype(jnp.bfloat16)
    sizes = {name: lax.axis_size(name) for name in DP_AXES}
    grad_pw2, _ = halving_scatter(contract_rows(hidden_full, cotangent), sizes, None)
    cot_full = lax.all_gather(cotangent, "mp", axis=1, tiled=True)
    weights_rows = lax.all_to_all(weights_two, "mp", split_axis=0, concat_axis=1, tiled=True)
    dhidden = lax.dot_general(
        cot_full, weights_rows, (((1,), (1,)), ((), ())), preferred_element_type=jnp.float32
    )
    dact = dhidden * valid_col * act_sig * (1.0 + act * (1.0 - act_sig))
    grad_bias, grad_gain = dp_sum((jnp.sum(dact, 0), jnp.sum(dact * normed_conv, 0)))
    dconv = (
        valid_col * inv_std * bn_gain * (dact - grad_bias / count - normed_conv * grad_gain / count)
    )
    kernel_part = kernel_terms(dconv, glu_out, kernel.shape[0], frames)
    dglu = depth_back(dconv, kernel, frames)
    dlin = dglu * valid_col * gate_sig
    dgate = dglu * valid_col * linear_part * gate_sig * (1.0 - gate_sig)
    dpre = jnp.concatenate([dlin, dgate], 1).astype(jnp.bfloat16)
    sizes = {name: lax.axis_size(name) for name in DP_AXES}
    width = dpre.shape[1]
    flat = kernel_part.reshape(-1)
    pad = (-flat.shape[0]) % width
    extra = jnp.pad(flat, (0, pad)).reshape(-1, width)
    grad_pw1, extra = halving_scatter(contract_rows(normed_full, dpre), sizes, extra)
    grad_kernel = extra.reshape(-1)[: flat.shape[0]].reshape(kernel_part.shape)
    grad_pw1 = grad_pw1.reshape(grad_pw1.shape[0], 2, half)
    return (encoded, grad_pw1, grad_pw2, grad_kernel, grad_gain, grad_bias)


def dp_shape(mesh):
    along = mesh.devices[:, 0]
    try:
        xs = len({d.coords[0] for d in along})
        ys = len({d.coords[1] for d in along})
    except AttributeError:
        xs, ys = 1, 1
    cores = mesh.shape["dp"] // (xs * ys)
    return xs, ys, cores


def solution(mesh):
    xs, ys, cores = dp_shape(mesh)
    fine = Mesh(
        mesh.devices.reshape(xs, ys, cores, mesh.shape["mp"]), DP_AXES + ("mp",)
    )
    D = DP_AXES
    return jax.shard_map(
        on_device,
        mesh=fine,
        in_specs=(
            P(D, None, None),
            P(D, None),
            P(D),
            P(D),
            P(None, "mp"),
            P(None, "mp"),
            P("mp"),
            P(D, None, "mp"),
            P(None, "mp"),
            P("mp"),
            P("mp"),
            P(D, "mp"),
            P(D, "mp"),
        ),
        out_specs=(
            P(D, "mp"),
            P(D, None, "mp"),
            P(D, "mp"),
            P(None, "mp"),
            P("mp"),
            P("mp"),
        ),
        check_vma=False,
    )
```

```python
import jax
import jax.numpy as jnp
from jax import lax
from jax.sharding import Mesh, PartitionSpec as P

EPS = 1e-05


def depth_conv(values, taps, frames):
    chans = values.shape[1]
    shaped = values.reshape(-1, frames, chans)
    margin = taps.shape[0] // 2
    padded = jnp.pad(shaped, ((0, 0), (margin, margin), (0, 0)))
    total = jnp.zeros(shaped.shape, jnp.float32)
    for step in range(taps.shape[0]):
        total = total + taps[step] * padded[:, step : step + frames]
    return total.reshape(values.shape)


def depth_back(grads, taps, frames):
    chans = grads.shape[1]
    shaped = grads.reshape(-1, frames, chans)
    margin = taps.shape[0] // 2
    padded = jnp.pad(shaped, ((0, 0), (margin, margin), (0, 0)))
    total = jnp.zeros(shaped.shape, jnp.float32)
    for step in range(taps.shape[0]):
        begin = 2 * margin - step
        total = total + taps[step] * padded[:, begin : begin + frames]
    return total.reshape(grads.shape)


def kernel_terms(grads, values, width, frames):
    chans = values.shape[1]
    shaped = values.reshape(-1, frames, chans)
    grad_shaped = grads.reshape(-1, frames, chans)
    margin = width // 2
    padded = jnp.pad(shaped, ((0, 0), (margin, margin), (0, 0)))
    rows_out = []
    for step in range(width):
        rows_out.append(jnp.sum(grad_shaped * padded[:, step : step + frames], axis=(0, 1)))
    return jnp.stack(rows_out, 0)


DP_AXES = ("x", "y", "c")


def dp_sum(value):
    for name in reversed(DP_AXES):
        value = lax.psum(value, name)
    return value


def dp_gather(value):
    for name in reversed(DP_AXES):
        value = lax.all_gather(value, name, axis=0, tiled=True)
    return value


def dp_scatter(value):
    for name in DP_AXES:
        value = lax.psum_scatter(value, name, scatter_dimension=0, tiled=True)
    return value


def halving_scatter(value, sizes, extra):
    cols = value.shape[1:]
    cur = value.reshape(tuple(sizes[a] for a in DP_AXES) + (-1,) + cols)
    rows = None if extra is None else extra.shape[0]
    for dim, name in reversed(list(enumerate(DP_AXES))):
        length = sizes[name]
        me = lax.axis_index(name)
        bit = length.bit_length() - 2
        while bit >= 0:
            shape = cur.shape
            span = shape[dim]
            split = shape[:dim] + (span >> (bit + 1), 2, 1 << bit) + shape[dim + 1 :]
            pieces = cur.reshape(split)
            mine = (me >> bit) & 1
            keep = lax.dynamic_index_in_dim(pieces, mine, dim + 1, keepdims=False)
            send = lax.dynamic_index_in_dim(pieces, 1 - mine, dim + 1, keepdims=False)
            perm = [(i, i ^ (1 << bit)) for i in range(length)]
            if extra is None:
                merged = keep + lax.ppermute(send, name, perm)
            else:
                message = jnp.concatenate([send.reshape((-1,) + cols), extra], 0)
                got = lax.ppermute(message, name, perm)
                merged = keep + got[:-rows].reshape(send.shape)
                extra = extra + got[-rows:]
            cur = merged.reshape(shape[:dim] + (span // 2,) + shape[dim + 1 :])
            bit -= 1
    return cur.reshape((-1,) + cols), extra


def doubling_gather(value, name):
    length = lax.axis_size(name)
    me = lax.axis_index(name)
    cur = value[None]
    bit = 0
    while (1 << bit) < length:
        perm = [(i, i ^ (1 << bit)) for i in range(length)]
        got = lax.ppermute(cur, name, perm)
        low = ((me >> bit) & 1) == 0
        cur = jnp.where(low, jnp.concatenate([cur, got]), jnp.concatenate([got, cur]))
        bit += 1
    return cur


def contract_rows(left, right):
    return lax.dot_general(
        left, right, (((0,), (0,)), ((), ())), preferred_element_type=jnp.float32
    )


def on_device(
    corpus,
    picks,
    lengths,
    langs,
    w_in,
    lang_table,
    ln_gain,
    w_pw1,
    kernel,
    bn_gain,
    bn_bias,
    w_pw2,
    cotangent,
):
    model_width = w_pw2.shape[0] * lax.axis_size(DP_AXES)
    chosen = picks[0]
    blocks = jnp.take(corpus, chosen, axis=0)
    meta_send = jnp.stack([jnp.take(lengths, chosen), jnp.take(langs, chosen)], 1)
    received = lax.all_to_all(blocks, DP_AXES, split_axis=0, concat_axis=0, tiled=True)
    meta = lax.all_to_all(meta_send, DP_AXES, split_axis=0, concat_axis=0, tiled=True)
    lens, lang = meta[:, 0], meta[:, 1]
    stacked = lax.all_gather(
        jnp.concatenate([w_pw1, w_pw2[:, None, :]], 1), DP_AXES, axis=0, tiled=True
    )
    frames = received.shape[1]
    valid = (
        (jnp.arange(frames, dtype=jnp.int32)[None, :] < lens[:, None])
        .astype(jnp.float32)
        .reshape(-1)
    )
    valid_col = valid[:, None]
    mel = received.reshape(-1, received.shape[2]) * valid_col.astype(jnp.bfloat16)
    onehot = (lang[:, None] == jnp.arange(lang_table.shape[0], dtype=jnp.int32)[None, :]).astype(
        jnp.bfloat16
    )
    feats = w_in.shape[0]
    tables = doubling_gather(jnp.concatenate([w_in, lang_table], 0), "mp")
    gains = doubling_gather(ln_gain, "mp").reshape(-1)
    parts, _, cols = tables.shape
    tables = jnp.transpose(tables, (1, 0, 2)).reshape(-1, parts * cols)
    w_in_full, lang_full = tables[:feats], tables[feats:]
    lang_rows = jnp.dot(onehot, lang_full, preferred_element_type=jnp.float32)
    inputs_full = jnp.dot(mel, w_in_full, preferred_element_type=jnp.float32) + jnp.repeat(
        lang_rows, frames, axis=0
    )
    mean = jnp.sum(inputs_full, 1) / model_width
    var = jnp.sum(inputs_full * inputs_full, 1) / model_width - mean * mean
    normed_full = (
        (inputs_full - mean[:, None]) * lax.rsqrt(var + EPS)[:, None] * gains
    ).astype(jnp.bfloat16)
    inputs = lax.dynamic_slice_in_dim(inputs_full, lax.axis_index("mp") * cols, cols, 1)
    weights_one = stacked[:, :2].reshape(model_width, -1)
    half = weights_one.shape[1] // 2
    pre = jnp.dot(normed_full, weights_one, preferred_element_type=jnp.float32)
    linear_part = pre[:, :half]
    gate_part = pre[:, half:]
    gate_sig = jax.nn.sigmoid(gate_part)
    glu_out = linear_part * gate_sig * valid_col
    conv_out = depth_conv(glu_out, kernel, frames)
    sum_conv, sum_sq, count = dp_sum(
        (
            jnp.sum(valid_col * conv_out, 0),
            jnp.sum(valid_col * conv_out * conv_out, 0),
            jnp.sum(valid),
        )
    )
    mu_conv = sum_conv / count
    var_conv = sum_sq / count - mu_conv * mu_conv
    inv_std = lax.rsqrt(var_conv + EPS)
    normed_conv = (conv_out - mu_conv) * inv_std
    act = normed_conv * bn_gain + bn_bias
    act_sig = jax.nn.sigmoid(act)
    hidden = (valid_col * act * act_sig).astype(jnp.bfloat16)
    weights_two = stacked[:, 2]
    hidden_parts = doubling_gather(hidden, "mp")
    hidden_full = jnp.transpose(hidden_parts, (1, 0, 2)).reshape(hidden.shape[0], -1)
    encoded = (
        inputs + jnp.dot(hidden_full, weights_two, preferred_element_type=jnp.float32)
    ).astype(jnp.bfloat16)
    sizes = {name: lax.axis_size(name) for name in DP_AXES}
    grad_pw2, _ = halving_scatter(contract_rows(hidden_full, cotangent), sizes, None)
    cot_full = lax.all_gather(cotangent, "mp", axis=1, tiled=True)
    weights_rows = lax.all_to_all(weights_two, "mp", split_axis=0, concat_axis=1, tiled=True)
    dhidden = lax.dot_general(
        cot_full, weights_rows, (((1,), (1,)), ((), ())), preferred_element_type=jnp.float32
    )
    dact = dhidden * valid_col * act_sig * (1.0 + act * (1.0 - act_sig))
    grad_bias, grad_gain = dp_sum((jnp.sum(dact, 0), jnp.sum(dact * normed_conv, 0)))
    dconv = (
        valid_col * inv_std * bn_gain * (dact - grad_bias / count - normed_conv * grad_gain / count)
    )
    kernel_part = kernel_terms(dconv, glu_out, kernel.shape[0], frames)
    dglu = depth_back(dconv, kernel, frames)
    dlin = dglu * valid_col * gate_sig
    dgate = dglu * valid_col * linear_part * gate_sig * (1.0 - gate_sig)
    dpre = jnp.concatenate([dlin, dgate], 1).astype(jnp.bfloat16)
    sizes = {name: lax.axis_size(name) for name in DP_AXES}
    width = dpre.shape[1]
    flat = kernel_part.reshape(-1)
    pad = (-flat.shape[0]) % width
    extra = jnp.pad(flat, (0, pad)).reshape(-1, width)
    grad_pw1, extra = halving_scatter(contract_rows(normed_full, dpre), sizes, extra)
    grad_kernel = extra.reshape(-1)[: flat.shape[0]].reshape(kernel_part.shape)
    grad_pw1 = grad_pw1.reshape(grad_pw1.shape[0], 2, half)
    return (encoded, grad_pw1, grad_pw2, grad_kernel, grad_gain, grad_bias)


def dp_shape(mesh):
    along = mesh.devices[:, 0]
    try:
        xs = len({d.coords[0] for d in along})
        ys = len({d.coords[1] for d in along})
    except AttributeError:
        xs, ys = 1, 1
    cores = mesh.shape["dp"] // (xs * ys)
    return xs, ys, cores


def solution(mesh):
    xs, ys, cores = dp_shape(mesh)
    fine = Mesh(
        mesh.devices.reshape(xs, ys, cores, mesh.shape["mp"]), DP_AXES + ("mp",)
    )
    D = DP_AXES
    return jax.shard_map(
        on_device,
        mesh=fine,
        in_specs=(
            P(D, None, None),
            P(D, None),
            P(D),
            P(D),
            P(None, "mp"),
            P(None, "mp"),
            P("mp"),
            P(D, None, "mp"),
            P(None, "mp"),
            P("mp"),
            P("mp"),
            P(D, "mp"),
            P(D, "mp"),
        ),
        out_specs=(
            P(D, "mp"),
            P(D, None, "mp"),
            P(D, "mp"),
            P(None, "mp"),
            P("mp"),
            P("mp"),
        ),
        check_vma=False,
    )
```

```python
import jax
import jax.numpy as jnp
from jax import lax
from jax.sharding import Mesh, PartitionSpec as P

EPS = 1e-05


def depth_conv(values, taps, frames):
    chans = values.shape[1]
    shaped = values.reshape(-1, frames, chans)
    margin = taps.shape[0] // 2
    padded = jnp.pad(shaped, ((0, 0), (margin, margin), (0, 0)))
    total = jnp.zeros(shaped.shape, jnp.float32)
    for step in range(taps.shape[0]):
        total = total + taps[step] * padded[:, step : step + frames]
    return total.reshape(values.shape)


def depth_back(grads, taps, frames):
    chans = grads.shape[1]
    shaped = grads.reshape(-1, frames, chans)
    margin = taps.shape[0] // 2
    padded = jnp.pad(shaped, ((0, 0), (margin, margin), (0, 0)))
    total = jnp.zeros(shaped.shape, jnp.float32)
    for step in range(taps.shape[0]):
        begin = 2 * margin - step
        total = total + taps[step] * padded[:, begin : begin + frames]
    return total.reshape(grads.shape)


def kernel_terms(grads, values, width, frames):
    chans = values.shape[1]
    shaped = values.reshape(-1, frames, chans)
    grad_shaped = grads.reshape(-1, frames, chans)
    margin = width // 2
    padded = jnp.pad(shaped, ((0, 0), (margin, margin), (0, 0)))
    rows_out = []
    for step in range(width):
        rows_out.append(jnp.sum(grad_shaped * padded[:, step : step + frames], axis=(0, 1)))
    return jnp.stack(rows_out, 0)


DP_AXES = ("x", "y", "c")


def dp_sum(value):
    for name in reversed(DP_AXES):
        value = lax.psum(value, name)
    return value


def dp_gather(value):
    for name in reversed(DP_AXES):
        value = lax.all_gather(value, name, axis=0, tiled=True)
    return value


def dp_scatter(value):
    for name in DP_AXES:
        value = lax.psum_scatter(value, name, scatter_dimension=0, tiled=True)
    return value


def halving_scatter(value, sizes, extra):
    cols = value.shape[1:]
    cur = value.reshape(tuple(sizes[a] for a in DP_AXES) + (-1,) + cols)
    rows = None if extra is None else extra.shape[0]
    for dim, name in reversed(list(enumerate(DP_AXES))):
        length = sizes[name]
        me = lax.axis_index(name)
        for bit in range(length.bit_length() - 1):
            shape = cur.shape
            span = shape[dim]
            split = shape[:dim] + (span // 2, 2) + shape[dim + 1 :]
            pieces = cur.reshape(split)
            mine = (me >> bit) & 1
            keep = lax.dynamic_index_in_dim(pieces, mine, dim + 1, keepdims=False)
            send = lax.dynamic_index_in_dim(pieces, 1 - mine, dim + 1, keepdims=False)
            perm = [(i, i ^ (1 << bit)) for i in range(length)]
            if extra is None:
                merged = keep + lax.ppermute(send, name, perm)
            else:
                message = jnp.concatenate([send.reshape((-1,) + cols), extra], 0)
                got = lax.ppermute(message, name, perm)
                merged = keep + got[:-rows].reshape(send.shape)
                extra = extra + got[-rows:]
            cur = merged.reshape(shape[:dim] + (span // 2,) + shape[dim + 1 :])
    return cur.reshape((-1,) + cols), extra


def doubling_gather(value, name):
    length = lax.axis_size(name)
    me = lax.axis_index(name)
    cur = value[None]
    bit = 0
    while (1 << bit) < length:
        perm = [(i, i ^ (1 << bit)) for i in range(length)]
        got = lax.ppermute(cur, name, perm)
        low = ((me >> bit) & 1) == 0
        cur = jnp.where(low, jnp.concatenate([cur, got]), jnp.concatenate([got, cur]))
        bit += 1
    return cur


def contract_rows(left, right):
    return lax.dot_general(
        left, right, (((0,), (0,)), ((), ())), preferred_element_type=jnp.float32
    )


def on_device(
    corpus,
    picks,
    lengths,
    langs,
    w_in,
    lang_table,
    ln_gain,
    w_pw1,
    kernel,
    bn_gain,
    bn_bias,
    w_pw2,
    cotangent,
):
    model_width = w_pw2.shape[0] * lax.axis_size(DP_AXES)
    chosen = picks[0]
    blocks = jnp.take(corpus, chosen, axis=0)
    meta_send = jnp.stack([jnp.take(lengths, chosen), jnp.take(langs, chosen)], 1)
    received = lax.all_to_all(blocks, DP_AXES, split_axis=0, concat_axis=0, tiled=True)
    meta = lax.all_to_all(meta_send, DP_AXES, split_axis=0, concat_axis=0, tiled=True)
    lens, lang = meta[:, 0], meta[:, 1]
    stacked = lax.all_gather(
        jnp.concatenate([w_pw1, w_pw2[:, None, :]], 1), DP_AXES, axis=0, tiled=True
    )
    frames = received.shape[1]
    valid = (
        (jnp.arange(frames, dtype=jnp.int32)[None, :] < lens[:, None])
        .astype(jnp.float32)
        .reshape(-1)
    )
    valid_col = valid[:, None]
    mel = received.reshape(-1, received.shape[2]) * valid_col.astype(jnp.bfloat16)
    onehot = (lang[:, None] == jnp.arange(lang_table.shape[0], dtype=jnp.int32)[None, :]).astype(
        jnp.bfloat16
    )
    feats = w_in.shape[0]
    tables = doubling_gather(jnp.concatenate([w_in, lang_table], 0), "mp")
    gains = doubling_gather(ln_gain, "mp").reshape(-1)
    parts, _, cols = tables.shape
    tables = jnp.transpose(tables, (1, 0, 2)).reshape(-1, parts * cols)
    w_in_full, lang_full = tables[:feats], tables[feats:]
    lang_rows = jnp.dot(onehot, lang_full, preferred_element_type=jnp.float32)
    inputs_full = jnp.dot(mel, w_in_full, preferred_element_type=jnp.float32) + jnp.repeat(
        lang_rows, frames, axis=0
    )
    mean = jnp.sum(inputs_full, 1) / model_width
    var = jnp.sum(inputs_full * inputs_full, 1) / model_width - mean * mean
    normed_full = (
        (inputs_full - mean[:, None]) * lax.rsqrt(var + EPS)[:, None] * gains
    ).astype(jnp.bfloat16)
    inputs = lax.dynamic_slice_in_dim(inputs_full, lax.axis_index("mp") * cols, cols, 1)
    weights_one = stacked[:, :2].reshape(model_width, -1)
    half = weights_one.shape[1] // 2
    pre = jnp.dot(normed_full, weights_one, preferred_element_type=jnp.float32)
    linear_part = pre[:, :half]
    gate_part = pre[:, half:]
    gate_sig = jax.nn.sigmoid(gate_part)
    glu_out = linear_part * gate_sig * valid_col
    conv_out = depth_conv(glu_out, kernel, frames)
    sum_conv, sum_sq, count = dp_sum(
        (
            jnp.sum(valid_col * conv_out, 0),
            jnp.sum(valid_col * conv_out * conv_out, 0),
            jnp.sum(valid),
        )
    )
    mu_conv = sum_conv / count
    var_conv = sum_sq / count - mu_conv * mu_conv
    inv_std = lax.rsqrt(var_conv + EPS)
    normed_conv = (conv_out - mu_conv) * inv_std
    act = normed_conv * bn_gain + bn_bias
    act_sig = jax.nn.sigmoid(act)
    hidden = (valid_col * act * act_sig).astype(jnp.bfloat16)
    weights_two = stacked[:, 2]
    hidden_full = lax.all_gather(hidden, "mp", axis=1, tiled=True)
    encoded = (
        inputs + jnp.dot(hidden_full, weights_two, preferred_element_type=jnp.float32)
    ).astype(jnp.bfloat16)
    sizes = {name: lax.axis_size(name) for name in DP_AXES}
    grad_pw2, _ = halving_scatter(contract_rows(hidden_full, cotangent), sizes, None)
    cot_full = lax.all_gather(cotangent, "mp", axis=1, tiled=True)
    weights_rows = lax.all_to_all(weights_two, "mp", split_axis=0, concat_axis=1, tiled=True)
    dhidden = lax.dot_general(
        cot_full, weights_rows, (((1,), (1,)), ((), ())), preferred_element_type=jnp.float32
    )
    dact = dhidden * valid_col * act_sig * (1.0 + act * (1.0 - act_sig))
    grad_bias, grad_gain = dp_sum((jnp.sum(dact, 0), jnp.sum(dact * normed_conv, 0)))
    dconv = (
        valid_col * inv_std * bn_gain * (dact - grad_bias / count - normed_conv * grad_gain / count)
    )
    kernel_part = kernel_terms(dconv, glu_out, kernel.shape[0], frames)
    dglu = depth_back(dconv, kernel, frames)
    dlin = dglu * valid_col * gate_sig
    dgate = dglu * valid_col * linear_part * gate_sig * (1.0 - gate_sig)
    dpre = jnp.concatenate([dlin, dgate], 1).astype(jnp.bfloat16)
    sizes = {name: lax.axis_size(name) for name in DP_AXES}
    width = dpre.shape[1]
    flat = kernel_part.reshape(-1)
    pad = (-flat.shape[0]) % width
    extra = jnp.pad(flat, (0, pad)).reshape(-1, width)
    grad_pw1, extra = halving_scatter(contract_rows(normed_full, dpre), sizes, extra)
    grad_kernel = extra.reshape(-1)[: flat.shape[0]].reshape(kernel_part.shape)
    grad_pw1 = grad_pw1.reshape(grad_pw1.shape[0], 2, half)
    return (encoded, grad_pw1, grad_pw2, grad_kernel, grad_gain, grad_bias)


def dp_shape(mesh):
    along = mesh.devices[:, 0]
    try:
        xs = len({d.coords[0] for d in along})
        ys = len({d.coords[1] for d in along})
    except AttributeError:
        xs, ys = 1, 1
    cores = mesh.shape["dp"] // (xs * ys)
    return xs, ys, cores


def solution(mesh):
    xs, ys, cores = dp_shape(mesh)
    fine = Mesh(
        mesh.devices.reshape(xs, ys, cores, mesh.shape["mp"]), DP_AXES + ("mp",)
    )
    D = DP_AXES
    return jax.shard_map(
        on_device,
        mesh=fine,
        in_specs=(
            P(D, None, None),
            P(D, None),
            P(D),
            P(D),
            P(None, "mp"),
            P(None, "mp"),
            P("mp"),
            P(D, None, "mp"),
            P(None, "mp"),
            P("mp"),
            P("mp"),
            P(D, "mp"),
            P(D, "mp"),
        ),
        out_specs=(
            P(D, "mp"),
            P(D, None, "mp"),
            P(D, "mp"),
            P(None, "mp"),
            P("mp"),
            P("mp"),
        ),
        check_vma=False,
    )
```

```python
import jax
import jax.numpy as jnp
from jax import lax
from jax.sharding import Mesh, PartitionSpec as P

EPS = 1e-05


def depth_conv(values, taps, frames):
    chans = values.shape[1]
    shaped = values.reshape(-1, frames, chans)
    margin = taps.shape[0] // 2
    padded = jnp.pad(shaped, ((0, 0), (margin, margin), (0, 0)))
    total = jnp.zeros(shaped.shape, jnp.float32)
    for step in range(taps.shape[0]):
        total = total + taps[step] * padded[:, step : step + frames]
    return total.reshape(values.shape)


def depth_back(grads, taps, frames):
    chans = grads.shape[1]
    shaped = grads.reshape(-1, frames, chans)
    margin = taps.shape[0] // 2
    padded = jnp.pad(shaped, ((0, 0), (margin, margin), (0, 0)))
    total = jnp.zeros(shaped.shape, jnp.float32)
    for step in range(taps.shape[0]):
        begin = 2 * margin - step
        total = total + taps[step] * padded[:, begin : begin + frames]
    return total.reshape(grads.shape)


def kernel_terms(grads, values, width, frames):
    chans = values.shape[1]
    shaped = values.reshape(-1, frames, chans)
    grad_shaped = grads.reshape(-1, frames, chans)
    margin = width // 2
    padded = jnp.pad(shaped, ((0, 0), (margin, margin), (0, 0)))
    rows_out = []
    for step in range(width):
        rows_out.append(jnp.sum(grad_shaped * padded[:, step : step + frames], axis=(0, 1)))
    return jnp.stack(rows_out, 0)


DP_AXES = ("x", "y", "c")


def dp_sum(value):
    for name in reversed(DP_AXES):
        value = lax.psum(value, name)
    return value


def dp_gather(value):
    for name in reversed(DP_AXES):
        value = lax.all_gather(value, name, axis=0, tiled=True)
    return value


def dp_scatter(value):
    for name in DP_AXES:
        value = lax.psum_scatter(value, name, scatter_dimension=0, tiled=True)
    return value


def halving_scatter(value, sizes, extra):
    cols = value.shape[1:]
    cur = value.reshape(tuple(sizes[a] for a in DP_AXES) + (-1,) + cols)
    rows = None if extra is None else extra.shape[0]
    steps = []
    for bit in range(max(n.bit_length() for n in sizes.values())):
        for dim, name in reversed(list(enumerate(DP_AXES))):
            if bit < sizes[name].bit_length() - 1:
                steps.append((dim, name, bit))
    for dim, name, bit in steps:
        length = sizes[name]
        me = lax.axis_index(name)
        if True:
            shape = cur.shape
            span = shape[dim]
            split = shape[:dim] + (span // 2, 2) + shape[dim + 1 :]
            pieces = cur.reshape(split)
            mine = (me >> bit) & 1
            keep = lax.dynamic_index_in_dim(pieces, mine, dim + 1, keepdims=False)
            send = lax.dynamic_index_in_dim(pieces, 1 - mine, dim + 1, keepdims=False)
            perm = [(i, i ^ (1 << bit)) for i in range(length)]
            if extra is None:
                merged = keep + lax.ppermute(send, name, perm)
            else:
                message = jnp.concatenate([send.reshape((-1,) + cols), extra], 0)
                got = lax.ppermute(message, name, perm)
                merged = keep + got[:-rows].reshape(send.shape)
                extra = extra + got[-rows:]
            cur = merged.reshape(shape[:dim] + (span // 2,) + shape[dim + 1 :])
    return cur.reshape((-1,) + cols), extra


def doubling_gather(value, name):
    length = lax.axis_size(name)
    me = lax.axis_index(name)
    cur = value[None]
    bit = 0
    while (1 << bit) < length:
        perm = [(i, i ^ (1 << bit)) for i in range(length)]
        got = lax.ppermute(cur, name, perm)
        low = ((me >> bit) & 1) == 0
        cur = jnp.where(low, jnp.concatenate([cur, got]), jnp.concatenate([got, cur]))
        bit += 1
    return cur


def contract_rows(left, right):
    return lax.dot_general(
        left, right, (((0,), (0,)), ((), ())), preferred_element_type=jnp.float32
    )


def on_device(
    corpus,
    picks,
    lengths,
    langs,
    w_in,
    lang_table,
    ln_gain,
    w_pw1,
    kernel,
    bn_gain,
    bn_bias,
    w_pw2,
    cotangent,
):
    model_width = w_pw2.shape[0] * lax.axis_size(DP_AXES)
    chosen = picks[0]
    blocks = jnp.take(corpus, chosen, axis=0)
    meta_send = jnp.stack([jnp.take(lengths, chosen), jnp.take(langs, chosen)], 1)
    received = lax.all_to_all(blocks, DP_AXES, split_axis=0, concat_axis=0, tiled=True)
    meta = lax.all_to_all(meta_send, DP_AXES, split_axis=0, concat_axis=0, tiled=True)
    lens, lang = meta[:, 0], meta[:, 1]
    stacked = lax.all_gather(
        jnp.concatenate([w_pw1, w_pw2[:, None, :]], 1), DP_AXES, axis=0, tiled=True
    )
    frames = received.shape[1]
    valid = (
        (jnp.arange(frames, dtype=jnp.int32)[None, :] < lens[:, None])
        .astype(jnp.float32)
        .reshape(-1)
    )
    valid_col = valid[:, None]
    mel = received.reshape(-1, received.shape[2]) * valid_col.astype(jnp.bfloat16)
    onehot = (lang[:, None] == jnp.arange(lang_table.shape[0], dtype=jnp.int32)[None, :]).astype(
        jnp.bfloat16
    )
    feats = w_in.shape[0]
    tables = doubling_gather(jnp.concatenate([w_in, lang_table], 0), "mp")
    gains = doubling_gather(ln_gain, "mp").reshape(-1)
    parts, _, cols = tables.shape
    tables = jnp.transpose(tables, (1, 0, 2)).reshape(-1, parts * cols)
    w_in_full, lang_full = tables[:feats], tables[feats:]
    lang_rows = jnp.dot(onehot, lang_full, preferred_element_type=jnp.float32)
    inputs_full = jnp.dot(mel, w_in_full, preferred_element_type=jnp.float32) + jnp.repeat(
        lang_rows, frames, axis=0
    )
    mean = jnp.sum(inputs_full, 1) / model_width
    var = jnp.sum(inputs_full * inputs_full, 1) / model_width - mean * mean
    normed_full = (
        (inputs_full - mean[:, None]) * lax.rsqrt(var + EPS)[:, None] * gains
    ).astype(jnp.bfloat16)
    inputs = lax.dynamic_slice_in_dim(inputs_full, lax.axis_index("mp") * cols, cols, 1)
    weights_one = stacked[:, :2].reshape(model_width, -1)
    half = weights_one.shape[1] // 2
    pre = jnp.dot(normed_full, weights_one, preferred_element_type=jnp.float32)
    linear_part = pre[:, :half]
    gate_part = pre[:, half:]
    gate_sig = jax.nn.sigmoid(gate_part)
    glu_out = linear_part * gate_sig * valid_col
    conv_out = depth_conv(glu_out, kernel, frames)
    sum_conv, sum_sq, count = dp_sum(
        (
            jnp.sum(valid_col * conv_out, 0),
            jnp.sum(valid_col * conv_out * conv_out, 0),
            jnp.sum(valid),
        )
    )
    mu_conv = sum_conv / count
    var_conv = sum_sq / count - mu_conv * mu_conv
    inv_std = lax.rsqrt(var_conv + EPS)
    normed_conv = (conv_out - mu_conv) * inv_std
    act = normed_conv * bn_gain + bn_bias
    act_sig = jax.nn.sigmoid(act)
    hidden = (valid_col * act * act_sig).astype(jnp.bfloat16)
    weights_two = stacked[:, 2]
    hidden_full = lax.all_gather(hidden, "mp", axis=1, tiled=True)
    encoded = (
        inputs + jnp.dot(hidden_full, weights_two, preferred_element_type=jnp.float32)
    ).astype(jnp.bfloat16)
    sizes = {name: lax.axis_size(name) for name in DP_AXES}
    grad_pw2, _ = halving_scatter(contract_rows(hidden_full, cotangent), sizes, None)
    cot_full = lax.all_gather(cotangent, "mp", axis=1, tiled=True)
    weights_rows = lax.all_to_all(weights_two, "mp", split_axis=0, concat_axis=1, tiled=True)
    dhidden = lax.dot_general(
        cot_full, weights_rows, (((1,), (1,)), ((), ())), preferred_element_type=jnp.float32
    )
    dact = dhidden * valid_col * act_sig * (1.0 + act * (1.0 - act_sig))
    grad_bias, grad_gain = dp_sum((jnp.sum(dact, 0), jnp.sum(dact * normed_conv, 0)))
    dconv = (
        valid_col * inv_std * bn_gain * (dact - grad_bias / count - normed_conv * grad_gain / count)
    )
    kernel_part = kernel_terms(dconv, glu_out, kernel.shape[0], frames)
    dglu = depth_back(dconv, kernel, frames)
    dlin = dglu * valid_col * gate_sig
    dgate = dglu * valid_col * linear_part * gate_sig * (1.0 - gate_sig)
    dpre = jnp.concatenate([dlin, dgate], 1).astype(jnp.bfloat16)
    sizes = {name: lax.axis_size(name) for name in DP_AXES}
    width = dpre.shape[1]
    flat = kernel_part.reshape(-1)
    pad = (-flat.shape[0]) % width
    extra = jnp.pad(flat, (0, pad)).reshape(-1, width)
    grad_pw1, extra = halving_scatter(contract_rows(normed_full, dpre), sizes, extra)
    grad_kernel = extra.reshape(-1)[: flat.shape[0]].reshape(kernel_part.shape)
    grad_pw1 = grad_pw1.reshape(grad_pw1.shape[0], 2, half)
    return (encoded, grad_pw1, grad_pw2, grad_kernel, grad_gain, grad_bias)


def dp_shape(mesh):
    along = mesh.devices[:, 0]
    try:
        xs = len({d.coords[0] for d in along})
        ys = len({d.coords[1] for d in along})
    except AttributeError:
        xs, ys = 1, 1
    cores = mesh.shape["dp"] // (xs * ys)
    return xs, ys, cores


def solution(mesh):
    xs, ys, cores = dp_shape(mesh)
    fine = Mesh(
        mesh.devices.reshape(xs, ys, cores, mesh.shape["mp"]), DP_AXES + ("mp",)
    )
    D = DP_AXES
    return jax.shard_map(
        on_device,
        mesh=fine,
        in_specs=(
            P(D, None, None),
            P(D, None),
            P(D),
            P(D),
            P(None, "mp"),
            P(None, "mp"),
            P("mp"),
            P(D, None, "mp"),
            P(None, "mp"),
            P("mp"),
            P("mp"),
            P(D, "mp"),
            P(D, "mp"),
        ),
        out_specs=(
            P(D, "mp"),
            P(D, None, "mp"),
            P(D, "mp"),
            P(None, "mp"),
            P("mp"),
            P("mp"),
        ),
        check_vma=False,
    )
```
